256 devices in a mesh: segment: 4 (over x_hi, core), dp: 64 (over y, x_lo, z).
Axes of the slice: x: 4 (x_hi: 2, x_lo: 2; x = x_hi * 2 + x_lo), y: 4, z: 8, core: 2. Of those that a mesh axis runs over, the one named last changes fastest.
Arguments:
- inputs: bfloat16 [8192, 4096], P('dp'), may hold values from -6 to 6
- cotangent: bfloat16 [8192, 4096], P('dp'), may hold values from -0.125 to 0.125
- blocks: bfloat16 [4, 32, 8, 128, 128], P('segment'), may hold values from -0.1875 to 0.1875
- block_cols: int32 [4, 32, 8], P('segment'), may hold values from 0 to 31, as said below
Outputs:
- grad_blocks: bfloat16 [4, 32768, 128], P('segment', 'dp')
The draws below stay inside these ranges and needn't reach their ends.
Inputs may be any that keep to these rules, and one draw needn't show every extreme that they name: In each layer, a row of block_cols names 8 different input blocks, and every input block is named exactly 8 times.
All inputs are finite; a program needn't handle non-finite values.
Results may differ from the reference program's by a relative error of at most 0.008.
Values may be sent and summed in bfloat16 or wider, within the bound.
No kernel may reach another device: no remote copies, remote signals or barrier semaphores. Data moves between devices by JAX's collectives and lax.ppermute only.
A program may use at most 128 MiB of HBM per device.

```python
import jax
import jax.numpy as jnp
from jax import lax

D = 4096
BLK = 128
KB = 8
ROWS_DEV = 128
NBLK = 32
LAYERS = 4
ROWS = 8192
N_DP = 64


def draw_block_cols(key, part):

    def one_layer(layer_key):
        key_perm, key_shift = jax.random.split(layer_key)
        shuffled = jax.random.permutation(key_perm, NBLK).astype(jnp.int32)
        offsets = (jax.random.permutation(key_shift, NBLK - 1)[:KB - 1] + 1).astype(jnp.int32)
        offsets = jnp.concatenate([jnp.zeros((1,), jnp.int32), offsets])
        return ((shuffled[:, None] + offsets[None, :]) % NBLK).astype(jnp.int32)
    layer_keys = jax.random.split(key, LAYERS)
    return jax.vmap(one_layer)(layer_keys)


def block_scale(key, dims, shards, low, largest):
    level, own = 1.0, jax.random.fold_in(key, 6)
    for axis_at, blocks in shards:
        heights = jnp.exp(jax.random.uniform(jax.random.fold_in(own, axis_at), (blocks,), jnp.float32, low / len(shards), largest / len(shards)))
        level = level * jnp.repeat(heights, dims[axis_at] // blocks).reshape([-1 if axis == axis_at else 1 for axis in range(len(dims))])
    return level


def centred(stream_key, dims, scale, most, pieces=(), held_as=jnp.bfloat16):
    array = scale * jax.random.normal(stream_key, dims, jnp.float32)
    if pieces:
        array = array * block_scale(stream_key, dims, pieces, -0.22, 0.18)
    return jnp.clip(array, -most, most).astype(held_as)


def setup_inputs(seed: int = 0) -> dict:
    arg_keys = jax.random.split(jax.random.key(seed), 5)
    inputs = centred(arg_keys[0], (ROWS, D), 1.0, 6.0, ((0, 64),))
    cotangent = centred(arg_keys[1], (ROWS, D), (2.0 / (ROWS_DEV * N_DP) ** 0.5), 0.125, ((0, 64),))
    blocks = centred(arg_keys[2], (LAYERS, NBLK, KB, BLK, BLK), (KB * BLK) ** -0.5, 0.1875, ((0, 4),))
    block_cols = draw_block_cols(jax.random.fold_in(arg_keys[4], 71), 0)
    return dict(inputs=inputs, cotangent=cotangent, blocks=blocks, block_cols=block_cols)


def forward_layer(hidden, weight, col_table):
    group_rows = hidden.shape[0]
    picked = hidden.reshape(group_rows, NBLK, BLK)[:, col_table.reshape(-1), :].reshape(group_rows, NBLK, KB, BLK)
    preact = jnp.einsum('rjka,jkab->rjb', picked.astype(jnp.float32), weight.astype(jnp.float32)).reshape(group_rows, D)
    return picked, preact


def reference(inputs, cotangent, blocks, block_cols):
    group_rows = ROWS_DEV

    def one_group(running, group_idx):
        row_start = (group_idx * group_rows).astype(jnp.int32)
        hidden = lax.dynamic_slice_in_dim(inputs, row_start, group_rows, 0)
        upstream = lax.dynamic_slice_in_dim(cotangent, row_start, group_rows, 0)
        stored = []
        for layer_idx in range(LAYERS):
            picked, preact = forward_layer(hidden, blocks[layer_idx], block_cols[layer_idx])
            stored.append((picked, preact))
            hidden = (hidden.astype(jnp.float32) + jax.nn.silu(preact)).astype(jnp.bfloat16)
        grad_list = []
        for layer_idx in reversed(range(LAYERS)):
            picked, preact = stored[layer_idx]
            sigmoid_z = jax.nn.sigmoid(preact)
            grad_pre = (upstream.astype(jnp.float32) * sigmoid_z * (1.0 + preact * (1.0 - sigmoid_z))).astype(jnp.bfloat16)
            grad_pre = grad_pre.reshape(group_rows, NBLK, BLK).astype(jnp.float32)
            grad_w = jnp.einsum('rjka,rjb->jkab', picked.astype(jnp.float32), grad_pre)
            contrib = jnp.einsum('rjb,jkab->rjka', grad_pre, blocks[layer_idx].astype(jnp.float32))
            contrib = contrib.reshape(group_rows, NBLK * KB, BLK)
            back_sum = jnp.zeros((group_rows, NBLK, BLK), jnp.float32).at[:, block_cols[layer_idx].reshape(-1), :].add(contrib)
            upstream = (upstream.astype(jnp.float32) + back_sum.reshape(group_rows, D)).astype(jnp.bfloat16)
            grad_list.append(grad_w)
        stacked = jnp.stack(grad_list[::-1])
        return running + stacked, None

    start_sum = jnp.zeros((LAYERS, NBLK, KB, BLK, BLK), jnp.float32)
    running, _ = lax.scan(one_group, start_sum, jnp.arange(N_DP, dtype=jnp.int32))
    return running.reshape(LAYERS, NBLK * KB * BLK, BLK).astype(jnp.bfloat16)
```

```python
import jax
import numpy as np
import jax.numpy as jnp
from jax import lax
from jax.sharding import Mesh, PartitionSpec as P

MICRO = 1
DP_AXES = ("y", "xlo", "z")
DP_SIZES = (4, 2, 8)


def from_behind(block, axis, distance):
    devices = range(lax.axis_size(axis))
    route = [(i - distance, i) for i in devices if i - distance in devices]
    return lax.ppermute(block, axis, route)


def body(inputs, cotangent, blocks, block_cols):
    segments = lax.axis_size("segment")
    segment_index = lax.axis_index("segment")
    groups = DP_SIZES[0] * DP_SIZES[1] * DP_SIZES[2]
    weight = blocks[0]
    col_table = block_cols[0]
    num_blocks, per_block, edge_size = (weight.shape[0], weight.shape[1], weight.shape[2])
    layer_width = inputs.shape[1]
    all_rows = inputs.shape[0]
    micro_rows = all_rows // MICRO
    tick_count = MICRO + segments - 1
    flat_cols = col_table.reshape(-1)
    pair_order = jnp.argsort(flat_cols, stable=True)
    source_block = (pair_order // per_block).reshape(num_blocks, per_block)
    sorted_weight = weight.reshape(num_blocks * per_block, edge_size, edge_size)[
        pair_order
    ].reshape(num_blocks, per_block, edge_size, edge_size)

    def picked_of(hidden, row_count):
        return hidden.reshape(row_count, num_blocks, edge_size)[:, flat_cols, :].reshape(
            row_count, num_blocks, per_block, edge_size
        )

    stash_x = jnp.zeros((MICRO, micro_rows, layer_width), jnp.bfloat16)
    stash_z = jnp.zeros((MICRO, micro_rows, layer_width), jnp.float32)
    arrived = jnp.zeros((micro_rows, layer_width), jnp.bfloat16)
    for step_now in range(tick_count):
        batch_index = step_now - segment_index
        active = (batch_index >= 0) & (batch_index < MICRO)
        position = jnp.clip(batch_index, 0, MICRO - 1)
        leading = lax.dynamic_slice_in_dim(inputs, position * micro_rows, micro_rows, 0)
        current = jnp.where(segment_index == 0, leading, arrived)
        preact = jnp.einsum(
            "rjka,jkab->rjb",
            picked_of(current, micro_rows),
            weight,
            preferred_element_type=jnp.float32,
        ).reshape(micro_rows, layer_width)
        result = (current.astype(jnp.float32) + jax.nn.silu(preact)).astype(jnp.bfloat16)
        old_x = lax.dynamic_index_in_dim(stash_x, position, 0, False)
        stash_x = lax.dynamic_update_index_in_dim(
            stash_x, jnp.where(active, current, old_x), position, 0
        )
        old_z = lax.dynamic_index_in_dim(stash_z, position, 0, False)
        stash_z = lax.dynamic_update_index_in_dim(
            stash_z, jnp.where(active, preact, old_z), position, 0
        )
        if step_now + 1 < tick_count:
            arrived = from_behind(result, "segment", 1)
    stash_g = jnp.zeros((MICRO, micro_rows, layer_width), jnp.bfloat16)
    incoming = jnp.zeros((micro_rows, layer_width), jnp.bfloat16)
    for step_now in range(tick_count):
        batch_index = step_now - (segments - 1 - segment_index)
        active = (batch_index >= 0) & (batch_index < MICRO)
        position = jnp.clip(batch_index, 0, MICRO - 1)
        from_cot = lax.dynamic_slice_in_dim(cotangent, position * micro_rows, micro_rows, 0)
        upstream = jnp.where(segment_index == segments - 1, from_cot, incoming)
        preact = lax.dynamic_index_in_dim(stash_z, position, 0, False)
        sigmoid_z = jax.nn.sigmoid(preact)
        grad_pre = (
            upstream.astype(jnp.float32) * sigmoid_z * (1.0 + preact * (1.0 - sigmoid_z))
        ).astype(jnp.bfloat16)
        old_g = lax.dynamic_index_in_dim(stash_g, position, 0, False)
        stash_g = lax.dynamic_update_index_in_dim(
            stash_g, jnp.where(active, grad_pre, old_g), position, 0
        )
        spread = grad_pre.reshape(micro_rows, num_blocks, edge_size)[:, source_block, :]
        back_sum = jnp.einsum(
            "rckb,ckab->rca", spread, sorted_weight, preferred_element_type=jnp.float32
        )
        passed = (upstream.astype(jnp.float32) + back_sum.reshape(micro_rows, layer_width)).astype(
            jnp.bfloat16
        )
        if step_now + 1 < tick_count:
            incoming = from_behind(passed, "segment", -1)
    all_inputs = stash_x.reshape(all_rows, layer_width)
    all_grads = stash_g.reshape(all_rows, layer_width)
    share_pairs = num_blocks * per_block // groups
    ny, nx, nz = DP_SIZES
    order = np.arange(num_blocks * per_block).reshape(ny, nx, nz, share_pairs)
    order = order.transpose(2, 0, 1, 3).reshape(-1)
    picked_cols = all_inputs.reshape(all_rows, num_blocks, edge_size)[:, flat_cols[order], :]
    grad_view = all_grads.reshape(all_rows, num_blocks, edge_size)
    chosen = grad_view[:, order // per_block, :]
    partial = jnp.einsum(
        "rpa,rpb->pab", picked_cols, chosen, preferred_element_type=jnp.float32
    ).reshape(num_blocks * per_block * edge_size, edge_size)
    for axis in ("z", "y", "xlo"):
        partial = lax.psum_scatter(partial, axis, scatter_dimension=0, tiled=True)
    own_share = partial
    summed = own_share.astype(jnp.bfloat16)
    return summed[None]


def solution(mesh):
    fine = Mesh(mesh.devices.reshape(mesh.shape["segment"], *DP_SIZES), ("segment",) + DP_AXES)
    return jax.shard_map(
        body,
        mesh=fine,
        in_specs=(
            P(DP_AXES, None),
            P(DP_AXES, None),
            P("segment", None, None, None, None),
            P("segment", None, None),
        ),
        out_specs=P("segment", DP_AXES, None),
        check_vma=False,
    )
```

```python
import jax
import numpy as np
import jax.numpy as jnp
from jax import lax
from jax.sharding import Mesh, PartitionSpec as P

MICRO = 1
DP_AXES = ("y", "xlo", "z")
DP_SIZES = (4, 2, 8)


def from_behind(block, axis, distance):
    devices = range(lax.axis_size(axis))
    route = [(i - distance, i) for i in devices if i - distance in devices]
    return lax.ppermute(block, axis, route)


def body(inputs, cotangent, blocks, block_cols):
    segments = lax.axis_size("segment")
    segment_index = lax.axis_index("segment")
    groups = DP_SIZES[0] * DP_SIZES[1] * DP_SIZES[2]
    weight = blocks[0]
    col_table = block_cols[0]
    num_blocks, per_block, edge_size = (weight.shape[0], weight.shape[1], weight.shape[2])
    layer_width = inputs.shape[1]
    all_rows = inputs.shape[0]
    micro_rows = all_rows // MICRO
    tick_count = MICRO + segments - 1
    flat_cols = col_table.reshape(-1)
    pair_order = jnp.argsort(flat_cols, stable=True)
    source_block = (pair_order // per_block).reshape(num_blocks, per_block)
    sorted_weight = weight.reshape(num_blocks * per_block, edge_size, edge_size)[
        pair_order
    ].reshape(num_blocks, per_block, edge_size, edge_size)

    def picked_of(hidden, row_count):
        return hidden.reshape(row_count, num_blocks, edge_size)[:, flat_cols, :].reshape(
            row_count, num_blocks, per_block, edge_size
        )

    stash_x = jnp.zeros((MICRO, micro_rows, layer_width), jnp.bfloat16)
    stash_z = jnp.zeros((MICRO, micro_rows, layer_width), jnp.float32)
    arrived = jnp.zeros((micro_rows, layer_width), jnp.bfloat16)
    for step_now in range(tick_count):
        batch_index = step_now - segment_index
        active = (batch_index >= 0) & (batch_index < MICRO)
        position = jnp.clip(batch_index, 0, MICRO - 1)
        leading = lax.dynamic_slice_in_dim(inputs, position * micro_rows, micro_rows, 0)
        current = jnp.where(segment_index == 0, leading, arrived)
        preact = jnp.einsum(
            "rjka,jkab->rjb",
            picked_of(current, micro_rows),
            weight,
            preferred_element_type=jnp.float32,
        ).reshape(micro_rows, layer_width)
        result = (current.astype(jnp.float32) + jax.nn.silu(preact)).astype(jnp.bfloat16)
        old_x = lax.dynamic_index_in_dim(stash_x, position, 0, False)
        stash_x = lax.dynamic_update_index_in_dim(
            stash_x, jnp.where(active, current, old_x), position, 0
        )
        old_z = lax.dynamic_index_in_dim(stash_z, position, 0, False)
        stash_z = lax.dynamic_update_index_in_dim(
            stash_z, jnp.where(active, preact, old_z), position, 0
        )
        if step_now + 1 < tick_count:
            arrived = from_behind(result, "segment", 1)
    stash_g = jnp.zeros((MICRO, micro_rows, layer_width), jnp.bfloat16)
    incoming = jnp.zeros((micro_rows, layer_width), jnp.bfloat16)
    for step_now in range(tick_count):
        batch_index = step_now - (segments - 1 - segment_index)
        active = (batch_index >= 0) & (batch_index < MICRO)
        position = jnp.clip(batch_index, 0, MICRO - 1)
        from_cot = lax.dynamic_slice_in_dim(cotangent, position * micro_rows, micro_rows, 0)
        upstream = jnp.where(segment_index == segments - 1, from_cot, incoming)
        preact = lax.dynamic_index_in_dim(stash_z, position, 0, False)
        sigmoid_z = jax.nn.sigmoid(preact)
        grad_pre = (
            upstream.astype(jnp.float32) * sigmoid_z * (1.0 + preact * (1.0 - sigmoid_z))
        ).astype(jnp.bfloat16)
        old_g = lax.dynamic_index_in_dim(stash_g, position, 0, False)
        stash_g = lax.dynamic_update_index_in_dim(
            stash_g, jnp.where(active, grad_pre, old_g), position, 0
        )
        spread = grad_pre.reshape(micro_rows, num_blocks, edge_size)[:, source_block, :]
        back_sum = jnp.einsum(
            "rckb,ckab->rca", spread, sorted_weight, preferred_element_type=jnp.float32
        )
        passed = (upstream.astype(jnp.float32) + back_sum.reshape(micro_rows, layer_width)).astype(
            jnp.bfloat16
        )
        if step_now + 1 < tick_count:
            incoming = from_behind(passed, "segment", -1)
    all_inputs = stash_x.reshape(all_rows, layer_width)
    all_grads = stash_g.reshape(all_rows, layer_width)
    ny, nx, nz = DP_SIZES
    members = ny * nx
    group_pairs = num_blocks * per_block // members
    group_j = num_blocks // members
    member = lax.axis_index("y") * nx + lax.axis_index("xlo")
    grads_here = all_grads.reshape(all_rows, members, group_j * edge_size)
    grads_group = lax.all_to_all(
        grads_here, ("y", "xlo"), split_axis=1, concat_axis=0, tiled=True
    ).reshape(members * all_rows, group_j, edge_size)
    inputs_group = lax.all_gather(all_inputs, ("y", "xlo"), axis=0, tiled=True)
    cols_here = lax.dynamic_slice_in_dim(flat_cols, member * group_pairs, group_pairs)
    picked_cols = inputs_group.reshape(members * all_rows, num_blocks, edge_size)[:, cols_here, :]
    chosen = grads_group[:, np.arange(group_pairs) // per_block, :]
    partial = jnp.einsum(
        "rpa,rpb->pab", picked_cols, chosen, preferred_element_type=jnp.float32
    ).reshape(group_pairs * edge_size, edge_size)
    own_share = lax.psum_scatter(partial, "z", scatter_dimension=0, tiled=True)
    summed = own_share.astype(jnp.bfloat16)
    return summed[None]


def solution(mesh):
    fine = Mesh(mesh.devices.reshape(mesh.shape["segment"], *DP_SIZES), ("segment",) + DP_AXES)
    return jax.shard_map(
        body,
        mesh=fine,
        in_specs=(
            P(DP_AXES, None),
            P(DP_AXES, None),
            P("segment", None, None, None, None),
            P("segment", None, None),
        ),
        out_specs=P("segment", DP_AXES, None),
        check_vma=False,
    )
```

```python
import functools

import jax
import jax.numpy as jnp
import numpy as np
from jax import lax
from jax.experimental import pallas as pl
from jax.experimental.pallas import tpu as pltpu
from jax.sharding import Mesh, PartitionSpec as P

DP_AXES = ("y", "xlo", "z")
DP_SIZES = (4, 2, 8)
JB = 4


def from_behind(block, axis, distance):
    devices = range(lax.axis_size(axis))
    route = [(i - distance, i) for i in devices if i - distance in devices]
    return lax.ppermute(block, axis, route)


def forward_kernel(cols_ref, h_ref, w_ref, z_ref, out_ref):
    edge = w_ref.shape[-1]
    per_block = w_ref.shape[1]
    step = pl.program_id(0)
    for jj in range(w_ref.shape[0]):
        j = step * w_ref.shape[0] + jj
        acc = None
        for k in range(per_block):
            c = cols_ref[j * per_block + k]
            x = h_ref[:, pl.ds(pl.multiple_of(c * edge, edge), edge)]
            part = jnp.dot(x, w_ref[jj, k], preferred_element_type=jnp.float32)
            acc = part if acc is None else acc + part
        z_ref[:, jj * edge:(jj + 1) * edge] = acc
        own = h_ref[:, pl.ds(pl.multiple_of(j * edge, edge), edge)].astype(jnp.float32)
        out_ref[:, jj * edge:(jj + 1) * edge] = (own + acc * jax.nn.sigmoid(acc)).astype(out_ref.dtype)


def backward_kernel(cols_ref, up_ref, z_ref, w_ref, g_ref, new_ref, back_ref):
    edge = w_ref.shape[-1]
    per_block = w_ref.shape[1]
    step = pl.program_id(0)

    @pl.when(step == 0)
    def _():
        back_ref[...] = jnp.zeros_like(back_ref)

    for jj in range(w_ref.shape[0]):
        j = step * w_ref.shape[0] + jj
        z = z_ref[:, jj * edge:(jj + 1) * edge]
        u = up_ref[:, pl.ds(pl.multiple_of(j * edge, edge), edge)].astype(jnp.float32)
        s = jax.nn.sigmoid(z)
        g = (u * s * (1.0 + z * (1.0 - s))).astype(jnp.bfloat16)
        g_ref[:, jj * edge:(jj + 1) * edge] = g
        for k in range(per_block):
            c = cols_ref[j * per_block + k]
            contrib = lax.dot_general(
                g, w_ref[jj, k], (((1,), (1,)), ((), ())), preferred_element_type=jnp.float32
            )
            at = pl.ds(pl.multiple_of(c * edge, edge), edge)
            back_ref[:, at] = back_ref[:, at] + contrib

    @pl.when(step == pl.num_programs(0) - 1)
    def _():
        new_ref[...] = (up_ref[...].astype(jnp.float32) + back_ref[...]).astype(new_ref.dtype)


def layer_forward(cols, hidden, weight):
    rows, width = hidden.shape
    num_blocks, per_block, edge, _ = weight.shape
    grid = pltpu.PrefetchScalarGridSpec(
        num_scalar_prefetch=1,
        grid=(num_blocks // JB,),
        in_specs=[
            pl.BlockSpec((rows, width), lambda i, c: (0, 0)),
            pl.BlockSpec((JB, per_block, edge, edge), lambda i, c: (i, 0, 0, 0)),
        ],
        out_specs=[
            pl.BlockSpec((rows, JB * edge), lambda i, c: (0, i)),
            pl.BlockSpec((rows, JB * edge), lambda i, c: (0, i)),
        ],
    )
    flops = 2 * rows * num_blocks * per_block * edge * edge
    return pl.pallas_call(
        forward_kernel,
        grid_spec=grid,
        out_shape=[
            jax.ShapeDtypeStruct((rows, width), jnp.float32),
            jax.ShapeDtypeStruct((rows, width), hidden.dtype),
        ],
        compiler_params=pltpu.CompilerParams(dimension_semantics=("arbitrary",)),
        cost_estimate=pl.CostEstimate(
            flops=flops, transcendentals=rows * width, bytes_accessed=weight.size * 2 + rows * width * 8
        ),
    )(cols, hidden, weight)


def layer_backward(cols, upstream, preact, weight):
    rows, width = upstream.shape
    num_blocks, per_block, edge, _ = weight.shape
    grid = pltpu.PrefetchScalarGridSpec(
        num_scalar_prefetch=1,
        grid=(num_blocks // JB,),
        in_specs=[
            pl.BlockSpec((rows, width), lambda i, c: (0, 0)),
            pl.BlockSpec((rows, JB * edge), lambda i, c: (0, i)),
            pl.BlockSpec((JB, per_block, edge, edge), lambda i, c: (i, 0, 0, 0)),
        ],
        out_specs=[
            pl.BlockSpec((rows, JB * edge), lambda i, c: (0, i)),
            pl.BlockSpec((rows, width), lambda i, c: (0, 0)),
        ],
        scratch_shapes=[pltpu.VMEM((rows, width), jnp.float32)],
    )
    flops = 2 * rows * num_blocks * per_block * edge * edge
    return pl.pallas_call(
        backward_kernel,
        grid_spec=grid,
        out_shape=[
            jax.ShapeDtypeStruct((rows, width), jnp.bfloat16),
            jax.ShapeDtypeStruct((rows, width), upstream.dtype),
        ],
        compiler_params=pltpu.CompilerParams(dimension_semantics=("arbitrary",)),
        cost_estimate=pl.CostEstimate(
            flops=flops, transcendentals=rows * width, bytes_accessed=weight.size * 2 + rows * width * 10
        ),
    )(cols, upstream, preact, weight)


def body(inputs, cotangent, blocks, block_cols):
    segments = lax.axis_size("segment")
    segment_index = lax.axis_index("segment")
    weight = blocks[0]
    num_blocks, per_block, edge_size = (weight.shape[0], weight.shape[1], weight.shape[2])
    all_rows, layer_width = inputs.shape
    flat_cols = block_cols[0].reshape(-1)

    stash_x = jnp.zeros((all_rows, layer_width), jnp.bfloat16)
    stash_z = jnp.zeros((all_rows, layer_width), jnp.float32)
    arrived = jnp.zeros((all_rows, layer_width), jnp.bfloat16)
    for step_now in range(segments):
        active = segment_index == step_now
        current = jnp.where(segment_index == 0, inputs, arrived)
        preact, result = layer_forward(flat_cols, current, weight)
        stash_x = jnp.where(active, current, stash_x)
        stash_z = jnp.where(active, preact, stash_z)
        if step_now + 1 < segments:
            arrived = from_behind(result, "segment", 1)
    stash_g = jnp.zeros((all_rows, layer_width), jnp.bfloat16)
    incoming = jnp.zeros((all_rows, layer_width), jnp.bfloat16)
    for step_now in range(segments):
        active = segment_index == segments - 1 - step_now
        upstream = jnp.where(segment_index == segments - 1, cotangent, incoming)
        grad_pre, passed = layer_backward(flat_cols, upstream, stash_z, weight)
        stash_g = jnp.where(active, grad_pre, stash_g)
        if step_now + 1 < segments:
            incoming = from_behind(passed, "segment", -1)
    all_inputs = stash_x
    all_grads = stash_g
    ny, nx, nz = DP_SIZES
    members = ny * nx
    group_pairs = num_blocks * per_block // members
    group_j = num_blocks // members
    member = lax.axis_index("y") * nx + lax.axis_index("xlo")
    grads_here = all_grads.reshape(all_rows, members, group_j * edge_size)
    grads_group = lax.all_to_all(
        grads_here, ("y", "xlo"), split_axis=1, concat_axis=0, tiled=True
    ).reshape(members * all_rows, group_j, edge_size)
    inputs_group = lax.all_gather(all_inputs, ("y", "xlo"), axis=0, tiled=True)
    cols_here = lax.dynamic_slice_in_dim(flat_cols, member * group_pairs, group_pairs)
    picked_cols = inputs_group.reshape(members * all_rows, num_blocks, edge_size)[:, cols_here, :]
    chosen = grads_group[:, np.arange(group_pairs) // per_block, :]
    partial = jnp.einsum(
        "rpa,rpb->pab", picked_cols, chosen, preferred_element_type=jnp.float32
    ).reshape(group_pairs * edge_size, edge_size)
    own_share = lax.psum_scatter(partial, "z", scatter_dimension=0, tiled=True)
    summed = own_share.astype(jnp.bfloat16)
    return summed[None]


def solution(mesh):
    fine = Mesh(mesh.devices.reshape(mesh.shape["segment"], *DP_SIZES), ("segment",) + DP_AXES)
    return jax.shard_map(
        body,
        mesh=fine,
        in_specs=(
            P(DP_AXES, None),
            P(DP_AXES, None),
            P("segment", None, None, None, None),
            P("segment", None, None),
        ),
        out_specs=P("segment", DP_AXES, None),
        check_vma=False,
    )
```

```python
import functools

import jax
import jax.numpy as jnp
import numpy as np
from jax import lax
from jax.experimental import pallas as pl
from jax.experimental.pallas import tpu as pltpu
from jax.sharding import Mesh, PartitionSpec as P

DP_AXES = ("y", "xlo", "z")
DP_SIZES = (4, 2, 8)
JB = 4
PER_BLOCK = 8


def from_behind(block, axis, distance):
    devices = range(lax.axis_size(axis))
    route = [(i - distance, i) for i in devices if i - distance in devices]
    return lax.ppermute(block, axis, route)


def forward_kernel(cols_ref, h_ref, w_ref, z_ref, out_ref):
    edge = w_ref.shape[-1]
    per_block = w_ref.shape[1]
    step = pl.program_id(0)
    for jj in range(w_ref.shape[0]):
        j = step * w_ref.shape[0] + jj
        acc = None
        for k in range(per_block):
            c = cols_ref[j * per_block + k]
            x = h_ref[:, pl.ds(pl.multiple_of(c * edge, edge), edge)]
            part = jnp.dot(x, w_ref[jj, k], preferred_element_type=jnp.float32)
            acc = part if acc is None else acc + part
        z_ref[:, jj * edge:(jj + 1) * edge] = acc
        own = h_ref[:, pl.ds(pl.multiple_of(j * edge, edge), edge)].astype(jnp.float32)
        out_ref[:, jj * edge:(jj + 1) * edge] = (own + acc * jax.nn.sigmoid(acc)).astype(out_ref.dtype)


def backward_kernel(cols_ref, up_ref, z_ref, w_ref, g_ref, new_ref, back_ref):
    edge = w_ref.shape[-1]
    per_block = w_ref.shape[1]
    step = pl.program_id(0)

    @pl.when(step == 0)
    def _():
        back_ref[...] = jnp.zeros_like(back_ref)

    for jj in range(w_ref.shape[0]):
        j = step * w_ref.shape[0] + jj
        z = z_ref[:, jj * edge:(jj + 1) * edge]
        u = up_ref[:, pl.ds(pl.multiple_of(j * edge, edge), edge)].astype(jnp.float32)
        s = jax.nn.sigmoid(z)
        g = (u * s * (1.0 + z * (1.0 - s))).astype(jnp.bfloat16)
        g_ref[:, jj * edge:(jj + 1) * edge] = g
        for k in range(per_block):
            c = cols_ref[j * per_block + k]
            contrib = lax.dot_general(
                g, w_ref[jj, k], (((1,), (1,)), ((), ())), preferred_element_type=jnp.float32
            )
            at = pl.ds(pl.multiple_of(c * edge, edge), edge)
            back_ref[:, at] = back_ref[:, at] + contrib

    @pl.when(step == pl.num_programs(0) - 1)
    def _():
        new_ref[...] = (up_ref[...].astype(jnp.float32) + back_ref[...]).astype(new_ref.dtype)


def layer_forward(cols, hidden, weight):
    rows, width = hidden.shape
    num_blocks, per_block, edge, _ = weight.shape
    grid = pltpu.PrefetchScalarGridSpec(
        num_scalar_prefetch=1,
        grid=(num_blocks // JB,),
        in_specs=[
            pl.BlockSpec((rows, width), lambda i, c: (0, 0)),
            pl.BlockSpec((JB, per_block, edge, edge), lambda i, c: (i, 0, 0, 0)),
        ],
        out_specs=[
            pl.BlockSpec((rows, JB * edge), lambda i, c: (0, i)),
            pl.BlockSpec((rows, JB * edge), lambda i, c: (0, i)),
        ],
    )
    flops = 2 * rows * num_blocks * per_block * edge * edge
    return pl.pallas_call(
        forward_kernel,
        grid_spec=grid,
        out_shape=[
            jax.ShapeDtypeStruct((rows, width), jnp.float32),
            jax.ShapeDtypeStruct((rows, width), hidden.dtype),
        ],
        compiler_params=pltpu.CompilerParams(dimension_semantics=("arbitrary",)),
        cost_estimate=pl.CostEstimate(
            flops=flops, transcendentals=rows * width, bytes_accessed=weight.size * 2 + rows * width * 8
        ),
    )(cols, hidden, weight)


def layer_backward(cols, upstream, preact, weight):
    rows, width = upstream.shape
    num_blocks, per_block, edge, _ = weight.shape
    grid = pltpu.PrefetchScalarGridSpec(
        num_scalar_prefetch=1,
        grid=(num_blocks // JB,),
        in_specs=[
            pl.BlockSpec((rows, width), lambda i, c: (0, 0)),
            pl.BlockSpec((rows, JB * edge), lambda i, c: (0, i)),
            pl.BlockSpec((JB, per_block, edge, edge), lambda i, c: (i, 0, 0, 0)),
        ],
        out_specs=[
            pl.BlockSpec((rows, JB * edge), lambda i, c: (0, i)),
            pl.BlockSpec((rows, width), lambda i, c: (0, 0)),
        ],
        scratch_shapes=[pltpu.VMEM((rows, width), jnp.float32)],
    )
    flops = 2 * rows * num_blocks * per_block * edge * edge
    return pl.pallas_call(
        backward_kernel,
        grid_spec=grid,
        out_shape=[
            jax.ShapeDtypeStruct((rows, width), jnp.bfloat16),
            jax.ShapeDtypeStruct((rows, width), upstream.dtype),
        ],
        compiler_params=pltpu.CompilerParams(dimension_semantics=("arbitrary",)),
        cost_estimate=pl.CostEstimate(
            flops=flops, transcendentals=rows * width, bytes_accessed=weight.size * 2 + rows * width * 10
        ),
    )(cols, upstream, preact, weight)


def grad_kernel(cols_ref, h_ref, g_ref, out_ref):
    edge = out_ref.shape[-1]
    per_step = out_ref.shape[0]
    step = pl.program_id(0)
    for qq in range(per_step):
        q = step * per_step + qq
        c = cols_ref[q]
        x = h_ref[:, pl.ds(pl.multiple_of(c * edge, edge), edge)]
        j = q // PER_BLOCK
        g = g_ref[:, pl.ds(pl.multiple_of(j * edge, edge), edge)]
        out_ref[qq] = lax.dot_general(
            x, g, (((0,), (0,)), ((), ())), preferred_element_type=jnp.float32
        )


def group_grads(cols, inputs_group, grads_group, pairs, per_step):
    rows, width = inputs_group.shape
    edge = 128
    grid = pltpu.PrefetchScalarGridSpec(
        num_scalar_prefetch=1,
        grid=(pairs // per_step,),
        in_specs=[
            pl.BlockSpec((rows, width), lambda i, c: (0, 0)),
            pl.BlockSpec(grads_group.shape, lambda i, c: (0, 0)),
        ],
        out_specs=pl.BlockSpec((per_step, edge, edge), lambda i, c: (i, 0, 0)),
    )
    return pl.pallas_call(
        grad_kernel,
        grid_spec=grid,
        out_shape=jax.ShapeDtypeStruct((pairs, edge, edge), jnp.float32),
        compiler_params=pltpu.CompilerParams(
            dimension_semantics=("arbitrary",), vmem_limit_bytes=48 * 1024 * 1024
        ),
        cost_estimate=pl.CostEstimate(
            flops=2 * rows * pairs * edge * edge,
            transcendentals=0,
            bytes_accessed=inputs_group.size * 2 + grads_group.size * 2 + pairs * edge * edge * 4,
        ),
    )(cols, inputs_group, grads_group)


def ring_reduce_scatter(chunks, axis, n):
    i = lax.axis_index(axis)
    half = chunks.shape[1] // 2
    east, west = chunks[:, :half], chunks[:, half:]
    cw = [(k, (k + 1) % n) for k in range(n)]
    ccw = [(k, (k - 1) % n) for k in range(n)]
    got_e = got_w = None
    for s in range(n - 1):
        send_e = lax.dynamic_index_in_dim(east, (i - s - 1) % n, 0, False)
        send_w = lax.dynamic_index_in_dim(west, (i + s + 1) % n, 0, False)
        if got_e is not None:
            send_e = got_e + send_e
            send_w = got_w + send_w
        got_e = lax.ppermute(send_e, axis, cw)
        got_w = lax.ppermute(send_w, axis, ccw)
    own_e = lax.dynamic_index_in_dim(east, i, 0, False)
    own_w = lax.dynamic_index_in_dim(west, i, 0, False)
    return jnp.concatenate([got_e + own_e, got_w + own_w], 0)


def body(inputs, cotangent, blocks, block_cols):
    segments = lax.axis_size("segment")
    segment_index = lax.axis_index("segment")
    weight = blocks[0]
    num_blocks, per_block, edge_size = (weight.shape[0], weight.shape[1], weight.shape[2])
    all_rows, layer_width = inputs.shape
    flat_cols = block_cols[0].reshape(-1)

    stash_x = jnp.zeros((all_rows, layer_width), jnp.bfloat16)
    stash_z = jnp.zeros((all_rows, layer_width), jnp.float32)
    arrived = jnp.zeros((all_rows, layer_width), jnp.bfloat16)
    for step_now in range(segments):
        active = segment_index == step_now
        current = jnp.where(segment_index == 0, inputs, arrived)
        preact, result = layer_forward(flat_cols, current, weight)
        stash_x = jnp.where(active, current, stash_x)
        stash_z = jnp.where(active, preact, stash_z)
        if step_now + 1 < segments:
            arrived = from_behind(result, "segment", 1)
    stash_g = jnp.zeros((all_rows, layer_width), jnp.bfloat16)
    incoming = jnp.zeros((all_rows, layer_width), jnp.bfloat16)
    for step_now in range(segments):
        active = segment_index == segments - 1 - step_now
        upstream = jnp.where(segment_index == segments - 1, cotangent, incoming)
        grad_pre, passed = layer_backward(flat_cols, upstream, stash_z, weight)
        stash_g = jnp.where(active, grad_pre, stash_g)
        if step_now + 1 < segments:
            incoming = from_behind(passed, "segment", -1)
    all_inputs = stash_x
    all_grads = stash_g
    ny, nx, nz = DP_SIZES
    members = ny * nx
    group_pairs = num_blocks * per_block // members
    group_j = num_blocks // members
    member = lax.axis_index("y") * nx + lax.axis_index("xlo")
    grads_here = all_grads.reshape(all_rows, members, group_j * edge_size)
    grads_group = lax.all_to_all(
        grads_here, ("y", "xlo"), split_axis=1, concat_axis=0, tiled=True
    ).reshape(members * all_rows, group_j, edge_size)
    inputs_group = lax.all_gather(all_inputs, ("y", "xlo"), axis=0, tiled=True)
    cols_here = lax.dynamic_slice_in_dim(flat_cols, member * group_pairs, group_pairs)
    grads_flat = grads_group.reshape(members * all_rows, group_j * edge_size)
    partial = group_grads(cols_here, inputs_group, grads_flat, group_pairs, group_pairs // nz)
    partial = partial.reshape(nz, group_pairs // nz * edge_size, edge_size)
    own_share = ring_reduce_scatter(partial, "z", nz)
    summed = own_share.astype(jnp.bfloat16)
    return summed[None]


def solution(mesh):
    fine = Mesh(mesh.devices.reshape(mesh.shape["segment"], *DP_SIZES), ("segment",) + DP_AXES)
    return jax.shard_map(
        body,
        mesh=fine,
        in_specs=(
            P(DP_AXES, None),
            P(DP_AXES, None),
            P("segment", None, None, None, None),
            P("segment", None, None),
        ),
        out_specs=P("segment", DP_AXES, None),
        check_vma=False,
    )
```

```python
import functools

import jax
import jax.numpy as jnp
import numpy as np
from jax import lax
from jax.experimental import pallas as pl
from jax.experimental.pallas import tpu as pltpu
from jax.sharding import Mesh, PartitionSpec as P

DP_AXES = ("y", "xlo", "z")
DP_SIZES = (4, 2, 8)
JB = 4
PER_BLOCK = 8


def from_behind(block, axis, distance):
    devices = range(lax.axis_size(axis))
    route = [(i - distance, i) for i in devices if i - distance in devices]
    return lax.ppermute(block, axis, route)


def forward_kernel(cols_ref, h_ref, w_ref, z_ref, out_ref):
    edge = w_ref.shape[-1]
    per_block = w_ref.shape[1]
    step = pl.program_id(0)
    for jj in range(w_ref.shape[0]):
        j = step * w_ref.shape[0] + jj
        acc = None
        for k in range(per_block):
            c = cols_ref[j * per_block + k]
            x = h_ref[:, pl.ds(pl.multiple_of(c * edge, edge), edge)]
            part = jnp.dot(x, w_ref[jj, k], preferred_element_type=jnp.float32)
            acc = part if acc is None else acc + part
        z_ref[:, jj * edge:(jj + 1) * edge] = acc
        own = h_ref[:, pl.ds(pl.multiple_of(j * edge, edge), edge)].astype(jnp.float32)
        out_ref[:, jj * edge:(jj + 1) * edge] = (own + acc * jax.nn.sigmoid(acc)).astype(out_ref.dtype)


def backward_kernel(cols_ref, up_ref, z_ref, w_ref, g_ref, new_ref, back_ref):
    edge = w_ref.shape[-1]
    per_block = w_ref.shape[1]
    step = pl.program_id(0)

    @pl.when(step == 0)
    def _():
        back_ref[...] = jnp.zeros_like(back_ref)

    for jj in range(w_ref.shape[0]):
        j = step * w_ref.shape[0] + jj
        z = z_ref[:, jj * edge:(jj + 1) * edge]
        u = up_ref[:, pl.ds(pl.multiple_of(j * edge, edge), edge)].astype(jnp.float32)
        s = jax.nn.sigmoid(z)
        g = (u * s * (1.0 + z * (1.0 - s))).astype(jnp.bfloat16)
        g_ref[:, jj * edge:(jj + 1) * edge] = g
        for k in range(per_block):
            c = cols_ref[j * per_block + k]
            contrib = lax.dot_general(
                g, w_ref[jj, k], (((1,), (1,)), ((), ())), preferred_element_type=jnp.float32
            )
            at = pl.ds(pl.multiple_of(c * edge, edge), edge)
            back_ref[:, at] = back_ref[:, at] + contrib

    @pl.when(step == pl.num_programs(0) - 1)
    def _():
        new_ref[...] = (up_ref[...].astype(jnp.float32) + back_ref[...]).astype(new_ref.dtype)


def layer_forward(cols, hidden, weight):
    rows, width = hidden.shape
    num_blocks, per_block, edge, _ = weight.shape
    grid = pltpu.PrefetchScalarGridSpec(
        num_scalar_prefetch=1,
        grid=(num_blocks // JB,),
        in_specs=[
            pl.BlockSpec((rows, width), lambda i, c: (0, 0)),
            pl.BlockSpec((JB, per_block, edge, edge), lambda i, c: (i, 0, 0, 0)),
        ],
        out_specs=[
            pl.BlockSpec((rows, JB * edge), lambda i, c: (0, i)),
            pl.BlockSpec((rows, JB * edge), lambda i, c: (0, i)),
        ],
    )
    flops = 2 * rows * num_blocks * per_block * edge * edge
    return pl.pallas_call(
        forward_kernel,
        grid_spec=grid,
        out_shape=[
            jax.ShapeDtypeStruct((rows, width), jnp.float32),
            jax.ShapeDtypeStruct((rows, width), hidden.dtype),
        ],
        compiler_params=pltpu.CompilerParams(dimension_semantics=("arbitrary",)),
        cost_estimate=pl.CostEstimate(
            flops=flops, transcendentals=rows * width, bytes_accessed=weight.size * 2 + rows * width * 8
        ),
    )(cols, hidden, weight)


def layer_backward(cols, upstream, preact, weight):
    rows, width = upstream.shape
    num_blocks, per_block, edge, _ = weight.shape
    grid = pltpu.PrefetchScalarGridSpec(
        num_scalar_prefetch=1,
        grid=(num_blocks // JB,),
        in_specs=[
            pl.BlockSpec((rows, width), lambda i, c: (0, 0)),
            pl.BlockSpec((rows, JB * edge), lambda i, c: (0, i)),
            pl.BlockSpec((JB, per_block, edge, edge), lambda i, c: (i, 0, 0, 0)),
        ],
        out_specs=[
            pl.BlockSpec((rows, JB * edge), lambda i, c: (0, i)),
            pl.BlockSpec((rows, width), lambda i, c: (0, 0)),
        ],
        scratch_shapes=[pltpu.VMEM((rows, width), jnp.float32)],
    )
    flops = 2 * rows * num_blocks * per_block * edge * edge
    return pl.pallas_call(
        backward_kernel,
        grid_spec=grid,
        out_shape=[
            jax.ShapeDtypeStruct((rows, width), jnp.bfloat16),
            jax.ShapeDtypeStruct((rows, width), upstream.dtype),
        ],
        compiler_params=pltpu.CompilerParams(dimension_semantics=("arbitrary",)),
        cost_estimate=pl.CostEstimate(
            flops=flops, transcendentals=rows * width, bytes_accessed=weight.size * 2 + rows * width * 10
        ),
    )(cols, upstream, preact, weight)


def grad_kernel(cols_ref, h_ref, g_ref, out_ref):
    edge = out_ref.shape[-1]
    per_step = out_ref.shape[0]
    step = pl.program_id(0)
    for qq in range(per_step):
        q = step * per_step + qq
        c = cols_ref[q]
        x = h_ref[:, pl.ds(pl.multiple_of(c * edge, edge), edge)]
        j = q // PER_BLOCK
        g = g_ref[:, pl.ds(pl.multiple_of(j * edge, edge), edge)]
        out_ref[qq] = lax.dot_general(
            x, g, (((0,), (0,)), ((), ())), preferred_element_type=jnp.float32
        )


def group_grads(cols, inputs_group, grads_group, pairs, per_step):
    rows, width = inputs_group.shape
    edge = 128
    grid = pltpu.PrefetchScalarGridSpec(
        num_scalar_prefetch=1,
        grid=(pairs // per_step,),
        in_specs=[
            pl.BlockSpec((rows, width), lambda i, c: (0, 0)),
            pl.BlockSpec(grads_group.shape, lambda i, c: (0, 0)),
        ],
        out_specs=pl.BlockSpec((per_step, edge, edge), lambda i, c: (i, 0, 0)),
    )
    return pl.pallas_call(
        grad_kernel,
        grid_spec=grid,
        out_shape=jax.ShapeDtypeStruct((pairs, edge, edge), jnp.float32),
        compiler_params=pltpu.CompilerParams(
            dimension_semantics=("arbitrary",), vmem_limit_bytes=48 * 1024 * 1024
        ),
        cost_estimate=pl.CostEstimate(
            flops=2 * rows * pairs * edge * edge,
            transcendentals=0,
            bytes_accessed=inputs_group.size * 2 + grads_group.size * 2 + pairs * edge * edge * 4,
        ),
    )(cols, inputs_group, grads_group)


def ring_reduce_scatter(chunks, axis, n):
    i = lax.axis_index(axis)
    half = chunks.shape[1] // 2
    east, west = chunks[:, :half], chunks[:, half:]
    cw = [(k, (k + 1) % n) for k in range(n)]
    ccw = [(k, (k - 1) % n) for k in range(n)]
    got_e = got_w = None
    for s in range(n - 1):
        send_e = lax.dynamic_index_in_dim(east, (i - s - 1) % n, 0, False)
        send_w = lax.dynamic_index_in_dim(west, (i + s + 1) % n, 0, False)
        if got_e is not None:
            send_e = got_e + send_e
            send_w = got_w + send_w
        got_e = lax.ppermute(send_e, axis, cw)
        got_w = lax.ppermute(send_w, axis, ccw)
    own_e = lax.dynamic_index_in_dim(east, i, 0, False)
    own_w = lax.dynamic_index_in_dim(west, i, 0, False)
    return jnp.concatenate([got_e + own_e, got_w + own_w], 0)


def body(inputs, cotangent, blocks, block_cols):
    segments = lax.axis_size("segment")
    segment_index = lax.axis_index("segment")
    weight = blocks[0]
    num_blocks, per_block, edge_size = (weight.shape[0], weight.shape[1], weight.shape[2])
    all_rows, layer_width = inputs.shape
    flat_cols = block_cols[0].reshape(-1)

    stash_x = jnp.zeros((all_rows, layer_width), jnp.bfloat16)
    stash_z = jnp.zeros((all_rows, layer_width), jnp.float32)
    arrived = jnp.zeros((all_rows, layer_width), jnp.bfloat16)
    for step_now in range(segments):
        active = segment_index == step_now
        current = jnp.where(segment_index == 0, inputs, arrived)
        preact, result = layer_forward(flat_cols, current, weight)
        stash_x = jnp.where(active, current, stash_x)
        stash_z = jnp.where(active, preact, stash_z)
        if step_now + 1 < segments:
            arrived = from_behind(result, "segment", 1)
    stash_g = jnp.zeros((all_rows, layer_width), jnp.bfloat16)
    incoming = jnp.zeros((all_rows, layer_width), jnp.bfloat16)
    for step_now in range(segments):
        active = segment_index == segments - 1 - step_now
        upstream = jnp.where(segment_index == segments - 1, cotangent, incoming)
        grad_pre, passed = layer_backward(flat_cols, upstream, stash_z, weight)
        stash_g = jnp.where(active, grad_pre, stash_g)
        if step_now + 1 < segments:
            incoming = from_behind(passed, "segment", -1)
    all_inputs = stash_x
    all_grads = stash_g
    ny, nx, nz = DP_SIZES
    members = ny
    group_pairs = num_blocks * per_block // members
    group_j = num_blocks // members
    member = lax.axis_index("y")
    grads_here = all_grads.reshape(all_rows, members, group_j * edge_size)
    grads_group = lax.all_to_all(
        grads_here, "y", split_axis=1, concat_axis=0, tiled=True
    ).reshape(members * all_rows, group_j * edge_size)
    inputs_group = lax.all_gather(all_inputs, "y", axis=0, tiled=True)
    cols_here = lax.dynamic_slice_in_dim(flat_cols, member * group_pairs, group_pairs)
    partial = group_grads(cols_here, inputs_group, grads_group, group_pairs, 8)
    halves = partial.reshape(nx, group_pairs // nx * edge_size, edge_size)
    side = lax.axis_index("xlo")
    got = lax.ppermute(lax.dynamic_index_in_dim(halves, 1 - side, 0, False), "xlo", [(0, 1), (1, 0)])
    kept = lax.dynamic_index_in_dim(halves, side, 0, False) + got
    own_share = ring_reduce_scatter(kept.reshape(nz, -1, edge_size), "z", nz)
    summed = own_share.astype(jnp.bfloat16)
    return summed[None]


def solution(mesh):
    fine = Mesh(mesh.devices.reshape(mesh.shape["segment"], *DP_SIZES), ("segment",) + DP_AXES)
    return jax.shard_map(
        body,
        mesh=fine,
        in_specs=(
            P(DP_AXES, None),
            P(DP_AXES, None),
            P("segment", None, None, None, None),
            P("segment", None, None),
        ),
        out_specs=P("segment", DP_AXES, None),
        check_vma=False,
    )
```

```python
import functools

import jax
import jax.numpy as jnp
import numpy as np
from jax import lax
from jax.experimental import pallas as pl
from jax.experimental.pallas import tpu as pltpu
from jax.sharding import Mesh, PartitionSpec as P

DP_AXES = ("y", "xlo", "z")
DP_SIZES = (4, 2, 8)
JB = 4
PER_BLOCK = 8


def from_behind(block, axis, distance):
    devices = range(lax.axis_size(axis))
    route = [(i - distance, i) for i in devices if i - distance in devices]
    return lax.ppermute(block, axis, route)


def forward_kernel(cols_ref, h_ref, w_ref, z_ref, out_ref):
    edge = w_ref.shape[-1]
    per_block = w_ref.shape[1]
    step = pl.program_id(0)
    for jj in range(w_ref.shape[0]):
        j = step * w_ref.shape[0] + jj
        picked = jnp.concatenate(
            [
                h_ref[:, pl.ds(pl.multiple_of(cols_ref[j * per_block + k] * edge, edge), edge)]
                for k in range(per_block)
            ],
            axis=1,
        )
        acc = jnp.dot(
            picked, w_ref[jj].reshape(per_block * edge, edge), preferred_element_type=jnp.float32
        )
        z_ref[:, jj * edge:(jj + 1) * edge] = acc
        own = h_ref[:, pl.ds(pl.multiple_of(j * edge, edge), edge)].astype(jnp.float32)
        out_ref[:, jj * edge:(jj + 1) * edge] = (own + acc * jax.nn.sigmoid(acc)).astype(out_ref.dtype)


def backward_kernel(cols_ref, up_ref, z_ref, w_ref, g_ref, new_ref, back_ref):
    edge = w_ref.shape[-1]
    per_block = w_ref.shape[1]
    step = pl.program_id(0)

    @pl.when(step == 0)
    def _():
        back_ref[...] = jnp.zeros_like(back_ref)

    for jj in range(w_ref.shape[0]):
        j = step * w_ref.shape[0] + jj
        z = z_ref[:, jj * edge:(jj + 1) * edge]
        u = up_ref[:, pl.ds(pl.multiple_of(j * edge, edge), edge)].astype(jnp.float32)
        s = jax.nn.sigmoid(z)
        g = (u * s * (1.0 + z * (1.0 - s))).astype(jnp.bfloat16)
        g_ref[:, jj * edge:(jj + 1) * edge] = g
        spread = lax.dot_general(
            g,
            w_ref[jj].reshape(per_block * edge, edge),
            (((1,), (1,)), ((), ())),
            preferred_element_type=jnp.float32,
        )
        for k in range(per_block):
            c = cols_ref[j * per_block + k]
            at = pl.ds(pl.multiple_of(c * edge, edge), edge)
            back_ref[:, at] = back_ref[:, at] + spread[:, k * edge:(k + 1) * edge]

    @pl.when(step == pl.num_programs(0) - 1)
    def _():
        new_ref[...] = (up_ref[...].astype(jnp.float32) + back_ref[...]).astype(new_ref.dtype)


def layer_forward(cols, hidden, weight):
    rows, width = hidden.shape
    num_blocks, per_block, edge, _ = weight.shape
    grid = pltpu.PrefetchScalarGridSpec(
        num_scalar_prefetch=1,
        grid=(num_blocks // JB,),
        in_specs=[
            pl.BlockSpec((rows, width), lambda i, c: (0, 0)),
            pl.BlockSpec((JB, per_block, edge, edge), lambda i, c: (i, 0, 0, 0)),
        ],
        out_specs=[
            pl.BlockSpec((rows, JB * edge), lambda i, c: (0, i)),
            pl.BlockSpec((rows, JB * edge), lambda i, c: (0, i)),
        ],
    )
    flops = 2 * rows * num_blocks * per_block * edge * edge
    return pl.pallas_call(
        forward_kernel,
        grid_spec=grid,
        out_shape=[
            jax.ShapeDtypeStruct((rows, width), jnp.float32),
            jax.ShapeDtypeStruct((rows, width), hidden.dtype),
        ],
        compiler_params=pltpu.CompilerParams(dimension_semantics=("arbitrary",)),
        cost_estimate=pl.CostEstimate(
            flops=flops, transcendentals=rows * width, bytes_accessed=weight.size * 2 + rows * width * 8
        ),
    )(cols, hidden, weight)


def layer_backward(cols, upstream, preact, weight):
    rows, width = upstream.shape
    num_blocks, per_block, edge, _ = weight.shape
    grid = pltpu.PrefetchScalarGridSpec(
        num_scalar_prefetch=1,
        grid=(num_blocks // JB,),
        in_specs=[
            pl.BlockSpec((rows, width), lambda i, c: (0, 0)),
            pl.BlockSpec((rows, JB * edge), lambda i, c: (0, i)),
            pl.BlockSpec((JB, per_block, edge, edge), lambda i, c: (i, 0, 0, 0)),
        ],
        out_specs=[
            pl.BlockSpec((rows, JB * edge), lambda i, c: (0, i)),
            pl.BlockSpec((rows, width), lambda i, c: (0, 0)),
        ],
        scratch_shapes=[pltpu.VMEM((rows, width), jnp.float32)],
    )
    flops = 2 * rows * num_blocks * per_block * edge * edge
    return pl.pallas_call(
        backward_kernel,
        grid_spec=grid,
        out_shape=[
            jax.ShapeDtypeStruct((rows, width), jnp.bfloat16),
            jax.ShapeDtypeStruct((rows, width), upstream.dtype),
        ],
        compiler_params=pltpu.CompilerParams(dimension_semantics=("arbitrary",)),
        cost_estimate=pl.CostEstimate(
            flops=flops, transcendentals=rows * width, bytes_accessed=weight.size * 2 + rows * width * 10
        ),
    )(cols, upstream, preact, weight)


def grad_kernel(cols_ref, h_ref, g_ref, out_ref):
    edge = out_ref.shape[-1]
    per_step = out_ref.shape[0]
    step = pl.program_id(0)
    for qq in range(per_step):
        q = step * per_step + qq
        c = cols_ref[q]
        x = h_ref[:, pl.ds(pl.multiple_of(c * edge, edge), edge)]
        j = q // PER_BLOCK
        g = g_ref[:, pl.ds(pl.multiple_of(j * edge, edge), edge)]
        out_ref[qq] = lax.dot_general(
            x, g, (((0,), (0,)), ((), ())), preferred_element_type=jnp.float32
        )


def group_grads(cols, inputs_group, grads_group, pairs, per_step):
    rows, width = inputs_group.shape
    edge = 128
    grid = pltpu.PrefetchScalarGridSpec(
        num_scalar_prefetch=1,
        grid=(pairs // per_step,),
        in_specs=[
            pl.BlockSpec((rows, width), lambda i, c: (0, 0)),
            pl.BlockSpec(grads_group.shape, lambda i, c: (0, 0)),
        ],
        out_specs=pl.BlockSpec((per_step, edge, edge), lambda i, c: (i, 0, 0)),
    )
    return pl.pallas_call(
        grad_kernel,
        grid_spec=grid,
        out_shape=jax.ShapeDtypeStruct((pairs, edge, edge), jnp.float32),
        compiler_params=pltpu.CompilerParams(
            dimension_semantics=("arbitrary",), vmem_limit_bytes=48 * 1024 * 1024
        ),
        cost_estimate=pl.CostEstimate(
            flops=2 * rows * pairs * edge * edge,
            transcendentals=0,
            bytes_accessed=inputs_group.size * 2 + grads_group.size * 2 + pairs * edge * edge * 4,
        ),
    )(cols, inputs_group, grads_group)


def ring_reduce_scatter(chunks, axis, n):
    i = lax.axis_index(axis)
    half = chunks.shape[1] // 2
    east, west = chunks[:, :half], chunks[:, half:]
    cw = [(k, (k + 1) % n) for k in range(n)]
    ccw = [(k, (k - 1) % n) for k in range(n)]
    got_e = got_w = None
    for s in range(n - 1):
        send_e = lax.dynamic_index_in_dim(east, (i - s - 1) % n, 0, False)
        send_w = lax.dynamic_index_in_dim(west, (i + s + 1) % n, 0, False)
        if got_e is not None:
            send_e = got_e + send_e
            send_w = got_w + send_w
        got_e = lax.ppermute(send_e, axis, cw)
        got_w = lax.ppermute(send_w, axis, ccw)
    own_e = lax.dynamic_index_in_dim(east, i, 0, False)
    own_w = lax.dynamic_index_in_dim(west, i, 0, False)
    return jnp.concatenate([got_e + own_e, got_w + own_w], 0)


def body(inputs, cotangent, blocks, block_cols):
    segments = lax.axis_size("segment")
    segment_index = lax.axis_index("segment")
    weight = blocks[0]
    num_blocks, per_block, edge_size = (weight.shape[0], weight.shape[1], weight.shape[2])
    all_rows, layer_width = inputs.shape
    flat_cols = block_cols[0].reshape(-1)

    stash_x = jnp.zeros((all_rows, layer_width), jnp.bfloat16)
    stash_z = jnp.zeros((all_rows, layer_width), jnp.float32)
    arrived = jnp.zeros((all_rows, layer_width), jnp.bfloat16)
    for step_now in range(segments):
        active = segment_index == step_now
        current = jnp.where(segment_index == 0, inputs, arrived)
        preact, result = layer_forward(flat_cols, current, weight)
        stash_x = jnp.where(active, current, stash_x)
        stash_z = jnp.where(active, preact, stash_z)
        if step_now + 1 < segments:
            arrived = from_behind(result, "segment", 1)
    stash_g = jnp.zeros((all_rows, layer_width), jnp.bfloat16)
    incoming = jnp.zeros((all_rows, layer_width), jnp.bfloat16)
    for step_now in range(segments):
        active = segment_index == segments - 1 - step_now
        upstream = jnp.where(segment_index == segments - 1, cotangent, incoming)
        grad_pre, passed = layer_backward(flat_cols, upstream, stash_z, weight)
        stash_g = jnp.where(active, grad_pre, stash_g)
        if step_now + 1 < segments:
            incoming = from_behind(passed, "segment", -1)
    all_inputs = stash_x
    all_grads = stash_g
    ny, nx, nz = DP_SIZES
    members = ny
    group_pairs = num_blocks * per_block // members
    group_j = num_blocks // members
    member = lax.axis_index("y")
    grads_here = all_grads.reshape(all_rows, members, group_j * edge_size)
    grads_group = lax.all_to_all(
        grads_here, "y", split_axis=1, concat_axis=0, tiled=True
    ).reshape(members * all_rows, group_j * edge_size)
    inputs_group = lax.all_gather(all_inputs, "y", axis=0, tiled=True)
    cols_here = lax.dynamic_slice_in_dim(flat_cols, member * group_pairs, group_pairs)
    partial = group_grads(cols_here, inputs_group, grads_group, group_pairs, 8)
    halves = partial.reshape(nx, group_pairs // nx * edge_size, edge_size)
    side = lax.axis_index("xlo")
    got = lax.ppermute(lax.dynamic_index_in_dim(halves, 1 - side, 0, False), "xlo", [(0, 1), (1, 0)])
    kept = lax.dynamic_index_in_dim(halves, side, 0, False) + got
    own_share = ring_reduce_scatter(kept.reshape(nz, -1, edge_size), "z", nz)
    summed = own_share.astype(jnp.bfloat16)
    return summed[None]


def solution(mesh):
    fine = Mesh(mesh.devices.reshape(mesh.shape["segment"], *DP_SIZES), ("segment",) + DP_AXES)
    return jax.shard_map(
        body,
        mesh=fine,
        in_specs=(
            P(DP_AXES, None),
            P(DP_AXES, None),
            P("segment", None, None, None, None),
            P("segment", None, None),
        ),
        out_specs=P("segment", DP_AXES, None),
        check_vma=False,
    )
```

```python
import functools

import jax
import jax.numpy as jnp
import numpy as np
from jax import lax
from jax.experimental import pallas as pl
from jax.experimental.pallas import tpu as pltpu
from jax.sharding import Mesh, PartitionSpec as P

DP_AXES = ("y", "xlo", "z")
DP_SIZES = (4, 2, 8)
JB = 4
PER_BLOCK = 8


def from_behind(block, axis, distance):
    devices = range(lax.axis_size(axis))
    route = [(i - distance, i) for i in devices if i - distance in devices]
    return lax.ppermute(block, axis, route)


def forward_kernel(cols_ref, h_ref, w_ref, z_ref, out_ref):
    edge = w_ref.shape[-1]
    per_block = w_ref.shape[1]
    step = pl.program_id(0)
    for jj in range(w_ref.shape[0]):
        j = step * w_ref.shape[0] + jj
        picked = jnp.concatenate(
            [
                h_ref[:, pl.ds(pl.multiple_of(cols_ref[j * per_block + k] * edge, edge), edge)]
                for k in range(per_block)
            ],
            axis=1,
        )
        acc = jnp.dot(
            picked, w_ref[jj].reshape(per_block * edge, edge), preferred_element_type=jnp.float32
        )
        z_ref[:, jj * edge:(jj + 1) * edge] = acc
        own = h_ref[:, pl.ds(pl.multiple_of(j * edge, edge), edge)].astype(jnp.float32)
        out_ref[:, jj * edge:(jj + 1) * edge] = (own + acc * jax.nn.sigmoid(acc)).astype(out_ref.dtype)


def backward_kernel(cols_ref, up_ref, z_ref, w_ref, g_ref, new_ref, back_ref):
    edge = w_ref.shape[-1]
    per_block = w_ref.shape[1]
    step = pl.program_id(0)

    @pl.when(step == 0)
    def _():
        back_ref[...] = jnp.zeros_like(back_ref)

    for jj in range(w_ref.shape[0]):
        j = step * w_ref.shape[0] + jj
        z = z_ref[:, jj * edge:(jj + 1) * edge]
        u = up_ref[:, pl.ds(pl.multiple_of(j * edge, edge), edge)].astype(jnp.float32)
        s = jax.nn.sigmoid(z)
        g = (u * s * (1.0 + z * (1.0 - s))).astype(jnp.bfloat16)
        g_ref[:, jj * edge:(jj + 1) * edge] = g
        spread = lax.dot_general(
            g,
            w_ref[jj].reshape(per_block * edge, edge),
            (((1,), (1,)), ((), ())),
            preferred_element_type=jnp.float32,
        )
        for k in range(per_block):
            c = cols_ref[j * per_block + k]
            at = pl.ds(pl.multiple_of(c * edge, edge), edge)
            back_ref[:, at] = back_ref[:, at] + spread[:, k * edge:(k + 1) * edge]

    @pl.when(step == pl.num_programs(0) - 1)
    def _():
        new_ref[...] = (up_ref[...].astype(jnp.float32) + back_ref[...]).astype(new_ref.dtype)


def layer_forward(cols, hidden, weight):
    rows, width = hidden.shape
    num_blocks, per_block, edge, _ = weight.shape
    grid = pltpu.PrefetchScalarGridSpec(
        num_scalar_prefetch=1,
        grid=(num_blocks // JB,),
        in_specs=[
            pl.BlockSpec((rows, width), lambda i, c: (0, 0)),
            pl.BlockSpec((JB, per_block, edge, edge), lambda i, c: (i, 0, 0, 0)),
        ],
        out_specs=[
            pl.BlockSpec((rows, JB * edge), lambda i, c: (0, i)),
            pl.BlockSpec((rows, JB * edge), lambda i, c: (0, i)),
        ],
    )
    flops = 2 * rows * num_blocks * per_block * edge * edge
    return pl.pallas_call(
        forward_kernel,
        grid_spec=grid,
        out_shape=[
            jax.ShapeDtypeStruct((rows, width), jnp.float32),
            jax.ShapeDtypeStruct((rows, width), hidden.dtype),
        ],
        compiler_params=pltpu.CompilerParams(dimension_semantics=("arbitrary",)),
        cost_estimate=pl.CostEstimate(
            flops=flops, transcendentals=rows * width, bytes_accessed=weight.size * 2 + rows * width * 8
        ),
    )(cols, hidden, weight)


def layer_backward(cols, upstream, preact, weight):
    rows, width = upstream.shape
    num_blocks, per_block, edge, _ = weight.shape
    grid = pltpu.PrefetchScalarGridSpec(
        num_scalar_prefetch=1,
        grid=(num_blocks // JB,),
        in_specs=[
            pl.BlockSpec((rows, width), lambda i, c: (0, 0)),
            pl.BlockSpec((rows, JB * edge), lambda i, c: (0, i)),
            pl.BlockSpec((JB, per_block, edge, edge), lambda i, c: (i, 0, 0, 0)),
        ],
        out_specs=[
            pl.BlockSpec((rows, JB * edge), lambda i, c: (0, i)),
            pl.BlockSpec((rows, width), lambda i, c: (0, 0)),
        ],
        scratch_shapes=[pltpu.VMEM((rows, width), jnp.float32)],
    )
    flops = 2 * rows * num_blocks * per_block * edge * edge
    return pl.pallas_call(
        backward_kernel,
        grid_spec=grid,
        out_shape=[
            jax.ShapeDtypeStruct((rows, width), jnp.bfloat16),
            jax.ShapeDtypeStruct((rows, width), upstream.dtype),
        ],
        compiler_params=pltpu.CompilerParams(dimension_semantics=("arbitrary",)),
        cost_estimate=pl.CostEstimate(
            flops=flops, transcendentals=rows * width, bytes_accessed=weight.size * 2 + rows * width * 10
        ),
    )(cols, upstream, preact, weight)


def grad_kernel(cols_ref, h_ref, g_ref, out_ref):
    edge = out_ref.shape[-1]
    per_step = out_ref.shape[0]
    step = pl.program_id(0)
    for qq in range(per_step):
        q = step * per_step + qq
        c = cols_ref[q]
        x = h_ref[:, pl.ds(pl.multiple_of(c * edge, edge), edge)]
        j = q // PER_BLOCK
        g = g_ref[:, pl.ds(pl.multiple_of(j * edge, edge), edge)]
        out_ref[qq] = lax.dot_general(
            x, g, (((0,), (0,)), ((), ())), preferred_element_type=jnp.float32
        )


def group_grads(cols, inputs_group, grads_group, pairs, per_step):
    rows, width = inputs_group.shape
    edge = 128
    grid = pltpu.PrefetchScalarGridSpec(
        num_scalar_prefetch=1,
        grid=(pairs // per_step,),
        in_specs=[
            pl.BlockSpec((rows, width), lambda i, c: (0, 0)),
            pl.BlockSpec(grads_group.shape, lambda i, c: (0, 0)),
        ],
        out_specs=pl.BlockSpec((per_step, edge, edge), lambda i, c: (i, 0, 0)),
    )
    return pl.pallas_call(
        grad_kernel,
        grid_spec=grid,
        out_shape=jax.ShapeDtypeStruct((pairs, edge, edge), jnp.float32),
        compiler_params=pltpu.CompilerParams(
            dimension_semantics=("arbitrary",), vmem_limit_bytes=48 * 1024 * 1024
        ),
        cost_estimate=pl.CostEstimate(
            flops=2 * rows * pairs * edge * edge,
            transcendentals=0,
            bytes_accessed=inputs_group.size * 2 + grads_group.size * 2 + pairs * edge * edge * 4,
        ),
    )(cols, inputs_group, grads_group)


def ring_reduce_scatter(chunks, axis, n):
    i = lax.axis_index(axis)
    half = chunks.shape[1] // 2
    east, west = chunks[:, :half], chunks[:, half:]
    cw = [(k, (k + 1) % n) for k in range(n)]
    ccw = [(k, (k - 1) % n) for k in range(n)]
    got_e = got_w = None
    for s in range(n - 1):
        send_e = lax.dynamic_index_in_dim(east, (i - s - 1) % n, 0, False)
        send_w = lax.dynamic_index_in_dim(west, (i + s + 1) % n, 0, False)
        if got_e is not None:
            send_e = got_e + send_e
            send_w = got_w + send_w
        got_e = lax.ppermute(send_e, axis, cw)
        got_w = lax.ppermute(send_w, axis, ccw)
    own_e = lax.dynamic_index_in_dim(east, i, 0, False)
    own_w = lax.dynamic_index_in_dim(west, i, 0, False)
    return jnp.concatenate([got_e + own_e, got_w + own_w], 0)


def body(inputs, cotangent, blocks, block_cols):
    segments = lax.axis_size("segment")
    segment_index = lax.axis_index("segment")
    weight = blocks[0]
    num_blocks, per_block, edge_size = (weight.shape[0], weight.shape[1], weight.shape[2])
    all_rows, layer_width = inputs.shape
    flat_cols = block_cols[0].reshape(-1)

    def hop(block, src, dst):
        return lax.ppermute(block, "segment", [(src, dst)])

    zeros_x = jnp.zeros((all_rows, layer_width), jnp.bfloat16)
    zeros_z = jnp.zeros((all_rows, layer_width), jnp.float32)
    stash_x = inputs
    stash_z = zeros_z
    current = inputs
    for step_now in range(segments):
        active = segment_index == step_now
        held = current
        stash_z, result = lax.cond(
            active,
            lambda: layer_forward(flat_cols, held, weight),
            lambda: (stash_z, zeros_x),
        )
        if step_now > 0:
            stash_x = jnp.where(active, current, stash_x)
        if step_now + 1 < segments:
            current = hop(result, step_now, step_now + 1)
    stash_g = zeros_x
    upstream = cotangent
    for step_now in range(segments):
        owner = segments - 1 - step_now
        active = segment_index == owner
        held = upstream
        stash_g, passed = lax.cond(
            active,
            lambda: layer_backward(flat_cols, held, stash_z, weight),
            lambda: (stash_g, zeros_x),
        )
        if step_now + 1 < segments:
            upstream = hop(passed, owner, owner - 1)
    all_inputs = stash_x
    all_grads = stash_g
    ny, nx, nz = DP_SIZES
    members = ny
    group_pairs = num_blocks * per_block // members
    group_j = num_blocks // members
    member = lax.axis_index("y")
    grads_here = all_grads.reshape(all_rows, members, group_j * edge_size)
    grads_group = lax.all_to_all(
        grads_here, "y", split_axis=1, concat_axis=0, tiled=True
    ).reshape(members * all_rows, group_j * edge_size)
    inputs_group = lax.all_gather(all_inputs, "y", axis=0, tiled=True)
    cols_here = lax.dynamic_slice_in_dim(flat_cols, member * group_pairs, group_pairs)
    partial = group_grads(cols_here, inputs_group, grads_group, group_pairs, 8)
    halves = partial.reshape(nx, group_pairs // nx * edge_size, edge_size)
    side = lax.axis_index("xlo")
    got = lax.ppermute(lax.dynamic_index_in_dim(halves, 1 - side, 0, False), "xlo", [(0, 1), (1, 0)])
    kept = lax.dynamic_index_in_dim(halves, side, 0, False) + got
    own_share = ring_reduce_scatter(kept.reshape(nz, -1, edge_size), "z", nz)
    summed = own_share.astype(jnp.bfloat16)
    return summed[None]


def solution(mesh):
    fine = Mesh(mesh.devices.reshape(mesh.shape["segment"], *DP_SIZES), ("segment",) + DP_AXES)
    return jax.shard_map(
        body,
        mesh=fine,
        in_specs=(
            P(DP_AXES, None),
            P(DP_AXES, None),
            P("segment", None, None, None, None),
            P("segment", None, None),
        ),
        out_specs=P("segment", DP_AXES, None),
        check_vma=False,
    )
```

```python
import functools

import jax
import jax.numpy as jnp
import numpy as np
from jax import lax
from jax.experimental import pallas as pl
from jax.experimental.pallas import tpu as pltpu
from jax.sharding import Mesh, PartitionSpec as P

DP_AXES = ("y", "xlo", "z")
DP_SIZES = (4, 2, 8)
JB = 4
PER_BLOCK = 8


def from_behind(block, axis, distance):
    devices = range(lax.axis_size(axis))
    route = [(i - distance, i) for i in devices if i - distance in devices]
    return lax.ppermute(block, axis, route)


def forward_kernel(cols_ref, h_ref, w_ref, z_ref, out_ref):
    edge = w_ref.shape[-1]
    per_block = w_ref.shape[1]
    step = pl.program_id(0)
    for jj in range(w_ref.shape[0]):
        j = step * w_ref.shape[0] + jj
        picked = jnp.concatenate(
            [
                h_ref[:, pl.ds(pl.multiple_of(cols_ref[j * per_block + k] * edge, edge), edge)]
                for k in range(per_block)
            ],
            axis=1,
        )
        acc = jnp.dot(
            picked, w_ref[jj].reshape(per_block * edge, edge), preferred_element_type=jnp.float32
        )
        z_ref[:, jj * edge:(jj + 1) * edge] = acc
        own = h_ref[:, pl.ds(pl.multiple_of(j * edge, edge), edge)].astype(jnp.float32)
        out_ref[:, jj * edge:(jj + 1) * edge] = (own + acc * jax.nn.sigmoid(acc)).astype(out_ref.dtype)


def backward_kernel(cols_ref, up_ref, z_ref, w_ref, g_ref, new_ref, back_ref):
    edge = w_ref.shape[-1]
    per_block = w_ref.shape[1]
    step = pl.program_id(0)

    @pl.when(step == 0)
    def _():
        back_ref[...] = jnp.zeros_like(back_ref)

    for jj in range(w_ref.shape[0]):
        j = step * w_ref.shape[0] + jj
        z = z_ref[:, jj * edge:(jj + 1) * edge]
        u = up_ref[:, pl.ds(pl.multiple_of(j * edge, edge), edge)].astype(jnp.float32)
        s = jax.nn.sigmoid(z)
        g = (u * s * (1.0 + z * (1.0 - s))).astype(jnp.bfloat16)
        g_ref[:, jj * edge:(jj + 1) * edge] = g
        spread = lax.dot_general(
            g,
            w_ref[jj].reshape(per_block * edge, edge),
            (((1,), (1,)), ((), ())),
            preferred_element_type=jnp.float32,
        )
        for k in range(per_block):
            c = cols_ref[j * per_block + k]
            at = pl.ds(pl.multiple_of(c * edge, edge), edge)
            back_ref[:, at] = back_ref[:, at] + spread[:, k * edge:(k + 1) * edge]

    @pl.when(step == pl.num_programs(0) - 1)
    def _():
        new_ref[...] = (up_ref[...].astype(jnp.float32) + back_ref[...]).astype(new_ref.dtype)


def layer_forward(cols, hidden, weight):
    rows, width = hidden.shape
    num_blocks, per_block, edge, _ = weight.shape
    grid = pltpu.PrefetchScalarGridSpec(
        num_scalar_prefetch=1,
        grid=(num_blocks // JB,),
        in_specs=[
            pl.BlockSpec((rows, width), lambda i, c: (0, 0)),
            pl.BlockSpec((JB, per_block, edge, edge), lambda i, c: (i, 0, 0, 0)),
        ],
        out_specs=[
            pl.BlockSpec((rows, JB * edge), lambda i, c: (0, i)),
            pl.BlockSpec((rows, JB * edge), lambda i, c: (0, i)),
        ],
    )
    flops = 2 * rows * num_blocks * per_block * edge * edge
    return pl.pallas_call(
        forward_kernel,
        grid_spec=grid,
        out_shape=[
            jax.ShapeDtypeStruct((rows, width), jnp.float32),
            jax.ShapeDtypeStruct((rows, width), hidden.dtype),
        ],
        compiler_params=pltpu.CompilerParams(dimension_semantics=("arbitrary",)),
        cost_estimate=pl.CostEstimate(
            flops=flops, transcendentals=rows * width, bytes_accessed=weight.size * 2 + rows * width * 8
        ),
    )(cols, hidden, weight)


def layer_backward(cols, upstream, preact, weight):
    rows, width = upstream.shape
    num_blocks, per_block, edge, _ = weight.shape
    grid = pltpu.PrefetchScalarGridSpec(
        num_scalar_prefetch=1,
        grid=(num_blocks // JB,),
        in_specs=[
            pl.BlockSpec((rows, width), lambda i, c: (0, 0)),
            pl.BlockSpec((rows, JB * edge), lambda i, c: (0, i)),
            pl.BlockSpec((JB, per_block, edge, edge), lambda i, c: (i, 0, 0, 0)),
        ],
        out_specs=[
            pl.BlockSpec((rows, JB * edge), lambda i, c: (0, i)),
            pl.BlockSpec((rows, width), lambda i, c: (0, 0)),
        ],
        scratch_shapes=[pltpu.VMEM((rows, width), jnp.float32)],
    )
    flops = 2 * rows * num_blocks * per_block * edge * edge
    return pl.pallas_call(
        backward_kernel,
        grid_spec=grid,
        out_shape=[
            jax.ShapeDtypeStruct((rows, width), jnp.bfloat16),
            jax.ShapeDtypeStruct((rows, width), upstream.dtype),
        ],
        compiler_params=pltpu.CompilerParams(dimension_semantics=("arbitrary",)),
        cost_estimate=pl.CostEstimate(
            flops=flops, transcendentals=rows * width, bytes_accessed=weight.size * 2 + rows * width * 10
        ),
    )(cols, upstream, preact, weight)


def grad_kernel(cols_ref, h_ref, g_ref, out_ref):
    edge = out_ref.shape[-1]
    per_step = out_ref.shape[0]
    step = pl.program_id(0)
    for qq in range(per_step):
        q = step * per_step + qq
        c = cols_ref[q]
        x = h_ref[:, pl.ds(pl.multiple_of(c * edge, edge), edge)]
        j = q // PER_BLOCK
        g = g_ref[:, pl.ds(pl.multiple_of(j * edge, edge), edge)]
        out_ref[qq] = lax.dot_general(
            x, g, (((0,), (0,)), ((), ())), preferred_element_type=jnp.float32
        )


def group_grads(cols, inputs_group, grads_group, pairs, per_step):
    rows, width = inputs_group.shape
    edge = 128
    grid = pltpu.PrefetchScalarGridSpec(
        num_scalar_prefetch=1,
        grid=(pairs // per_step,),
        in_specs=[
            pl.BlockSpec((rows, width), lambda i, c: (0, 0)),
            pl.BlockSpec(grads_group.shape, lambda i, c: (0, 0)),
        ],
        out_specs=pl.BlockSpec((per_step, edge, edge), lambda i, c: (i, 0, 0)),
    )
    return pl.pallas_call(
        grad_kernel,
        grid_spec=grid,
        out_shape=jax.ShapeDtypeStruct((pairs, edge, edge), jnp.float32),
        compiler_params=pltpu.CompilerParams(
            dimension_semantics=("arbitrary",), vmem_limit_bytes=48 * 1024 * 1024
        ),
        cost_estimate=pl.CostEstimate(
            flops=2 * rows * pairs * edge * edge,
            transcendentals=0,
            bytes_accessed=inputs_group.size * 2 + grads_group.size * 2 + pairs * edge * edge * 4,
        ),
    )(cols, inputs_group, grads_group)


def ring_reduce_scatter(chunks, axis, n):
    i = lax.axis_index(axis)
    half = chunks.shape[1] // 2
    east, west = chunks[:, :half], chunks[:, half:]
    cw = [(k, (k + 1) % n) for k in range(n)]
    ccw = [(k, (k - 1) % n) for k in range(n)]
    got_e = got_w = None
    for s in range(n - 1):
        send_e = lax.dynamic_index_in_dim(east, (i - s - 1) % n, 0, False)
        send_w = lax.dynamic_index_in_dim(west, (i + s + 1) % n, 0, False)
        if got_e is not None:
            send_e = got_e + send_e
            send_w = got_w + send_w
        got_e = lax.ppermute(send_e, axis, cw)
        got_w = lax.ppermute(send_w, axis, ccw)
    own_e = lax.dynamic_index_in_dim(east, i, 0, False)
    own_w = lax.dynamic_index_in_dim(west, i, 0, False)
    return jnp.concatenate([got_e + own_e, got_w + own_w], 0)


def body(inputs, cotangent, blocks, block_cols):
    segments = lax.axis_size("segment")
    segment_index = lax.axis_index("segment")
    weight = blocks[0]
    num_blocks, per_block, edge_size = (weight.shape[0], weight.shape[1], weight.shape[2])
    all_rows, layer_width = inputs.shape
    flat_cols = block_cols[0].reshape(-1)

    sides = DP_SIZES[1]
    middle = segments // 2

    def hop(block, src, dst):
        flip = (src < middle) != (dst < middle)
        route = [(src * sides + x, dst * sides + (sides - 1 - x if flip else x)) for x in range(sides)]
        return lax.ppermute(block, ("segment", "xlo"), route)

    zeros_x = jnp.zeros((all_rows, layer_width), jnp.bfloat16)
    zeros_z = jnp.zeros((all_rows, layer_width), jnp.float32)
    stash_x = inputs
    stash_z = zeros_z
    current = inputs
    for step_now in range(segments):
        active = segment_index == step_now
        held = current
        stash_z, result = lax.cond(
            active,
            lambda: layer_forward(flat_cols, held, weight),
            lambda: (stash_z, zeros_x),
        )
        if step_now > 0:
            stash_x = jnp.where(active, current, stash_x)
        if step_now + 1 < segments:
            current = hop(result, step_now, step_now + 1)
    stash_g = zeros_x
    last = segments - 1
    upstream = lax.ppermute(
        cotangent, ("segment", "xlo"), [(last * sides + x, last * sides + sides - 1 - x) for x in range(sides)]
    )
    for step_now in range(segments):
        owner = segments - 1 - step_now
        active = segment_index == owner
        held = upstream
        stash_g, passed = lax.cond(
            active,
            lambda: layer_backward(flat_cols, held, stash_z, weight),
            lambda: (stash_g, zeros_x),
        )
        if step_now + 1 < segments:
            upstream = hop(passed, owner, owner - 1)
    all_inputs = stash_x
    all_grads = stash_g
    ny, nx, nz = DP_SIZES
    members = ny * nx
    group_pairs = num_blocks * per_block // members
    group_j = num_blocks // members
    member = lax.axis_index("y") * nx + lax.axis_index("xlo")
    grads_here = all_grads.reshape(all_rows, members, group_j * edge_size)
    grads_group = lax.all_to_all(
        grads_here, ("y", "xlo"), split_axis=1, concat_axis=0, tiled=True
    ).reshape(members * all_rows, group_j * edge_size)
    inputs_group = lax.all_gather(all_inputs, ("y", "xlo"), axis=0, tiled=True)
    cols_here = lax.dynamic_slice_in_dim(flat_cols, member * group_pairs, group_pairs)
    partial = group_grads(cols_here, inputs_group, grads_group, group_pairs, group_pairs // nz)
    own_share = ring_reduce_scatter(partial.reshape(nz, -1, edge_size), "z", nz)
    summed = own_share.astype(jnp.bfloat16)
    return summed[None]


def solution(mesh):
    fine = Mesh(mesh.devices.reshape(mesh.shape["segment"], *DP_SIZES), ("segment",) + DP_AXES)
    return jax.shard_map(
        body,
        mesh=fine,
        in_specs=(
            P(DP_AXES, None),
            P(DP_AXES, None),
            P("segment", None, None, None, None),
            P("segment", None, None),
        ),
        out_specs=P("segment", DP_AXES, None),
        check_vma=False,
    )
```

```python
import functools

import jax
import jax.numpy as jnp
import numpy as np
from jax import lax
from jax.experimental import pallas as pl
from jax.experimental.pallas import tpu as pltpu
from jax.sharding import Mesh, PartitionSpec as P

DP_AXES = ("y", "xlo", "z")
DP_SIZES = (4, 2, 8)
JB = 8
PER_BLOCK = 8


def from_behind(block, axis, distance):
    devices = range(lax.axis_size(axis))
    route = [(i - distance, i) for i in devices if i - distance in devices]
    return lax.ppermute(block, axis, route)


def forward_kernel(cols_ref, h_ref, w_ref, z_ref, out_ref):
    edge = w_ref.shape[-1]
    per_block = w_ref.shape[1]
    step = pl.program_id(0)
    for jj in range(w_ref.shape[0]):
        j = step * w_ref.shape[0] + jj
        picked = jnp.concatenate(
            [
                h_ref[:, pl.ds(pl.multiple_of(cols_ref[j * per_block + k] * edge, edge), edge)]
                for k in range(per_block)
            ],
            axis=1,
        )
        acc = jnp.dot(
            picked, w_ref[jj].reshape(per_block * edge, edge), preferred_element_type=jnp.float32
        )
        z_ref[:, jj * edge:(jj + 1) * edge] = acc
        own = h_ref[:, pl.ds(pl.multiple_of(j * edge, edge), edge)].astype(jnp.float32)
        out_ref[:, jj * edge:(jj + 1) * edge] = (own + acc * jax.nn.sigmoid(acc)).astype(out_ref.dtype)


def backward_kernel(cols_ref, up_ref, z_ref, w_ref, g_ref, new_ref, back_ref):
    edge = w_ref.shape[-1]
    per_block = w_ref.shape[1]
    step = pl.program_id(0)

    @pl.when(step == 0)
    def _():
        back_ref[...] = jnp.zeros_like(back_ref)

    for jj in range(w_ref.shape[0]):
        j = step * w_ref.shape[0] + jj
        z = z_ref[:, jj * edge:(jj + 1) * edge]
        u = up_ref[:, pl.ds(pl.multiple_of(j * edge, edge), edge)].astype(jnp.float32)
        s = jax.nn.sigmoid(z)
        g = (u * s * (1.0 + z * (1.0 - s))).astype(jnp.bfloat16)
        g_ref[:, jj * edge:(jj + 1) * edge] = g
        spread = lax.dot_general(
            g,
            w_ref[jj].reshape(per_block * edge, edge),
            (((1,), (1,)), ((), ())),
            preferred_element_type=jnp.float32,
        )
        for k in range(per_block):
            c = cols_ref[j * per_block + k]
            at = pl.ds(pl.multiple_of(c * edge, edge), edge)
            back_ref[:, at] = back_ref[:, at] + spread[:, k * edge:(k + 1) * edge]

    @pl.when(step == pl.num_programs(0) - 1)
    def _():
        new_ref[...] = (up_ref[...].astype(jnp.float32) + back_ref[...]).astype(new_ref.dtype)


def layer_forward(cols, hidden, weight):
    rows, width = hidden.shape
    num_blocks, per_block, edge, _ = weight.shape
    grid = pltpu.PrefetchScalarGridSpec(
        num_scalar_prefetch=1,
        grid=(num_blocks // JB,),
        in_specs=[
            pl.BlockSpec((rows, width), lambda i, c: (0, 0)),
            pl.BlockSpec((JB, per_block, edge, edge), lambda i, c: (i, 0, 0, 0)),
        ],
        out_specs=[
            pl.BlockSpec((rows, JB * edge), lambda i, c: (0, i)),
            pl.BlockSpec((rows, JB * edge), lambda i, c: (0, i)),
        ],
    )
    flops = 2 * rows * num_blocks * per_block * edge * edge
    return pl.pallas_call(
        forward_kernel,
        grid_spec=grid,
        out_shape=[
            jax.ShapeDtypeStruct((rows, width), jnp.float32),
            jax.ShapeDtypeStruct((rows, width), hidden.dtype),
        ],
        compiler_params=pltpu.CompilerParams(dimension_semantics=("arbitrary",)),
        cost_estimate=pl.CostEstimate(
            flops=flops, transcendentals=rows * width, bytes_accessed=weight.size * 2 + rows * width * 8
        ),
    )(cols, hidden, weight)


def layer_backward(cols, upstream, preact, weight):
    rows, width = upstream.shape
    num_blocks, per_block, edge, _ = weight.shape
    grid = pltpu.PrefetchScalarGridSpec(
        num_scalar_prefetch=1,
        grid=(num_blocks // JB,),
        in_specs=[
            pl.BlockSpec((rows, width), lambda i, c: (0, 0)),
            pl.BlockSpec((rows, JB * edge), lambda i, c: (0, i)),
            pl.BlockSpec((JB, per_block, edge, edge), lambda i, c: (i, 0, 0, 0)),
        ],
        out_specs=[
            pl.BlockSpec((rows, JB * edge), lambda i, c: (0, i)),
            pl.BlockSpec((rows, width), lambda i, c: (0, 0)),
        ],
        scratch_shapes=[pltpu.VMEM((rows, width), jnp.float32)],
    )
    flops = 2 * rows * num_blocks * per_block * edge * edge
    return pl.pallas_call(
        backward_kernel,
        grid_spec=grid,
        out_shape=[
            jax.ShapeDtypeStruct((rows, width), jnp.bfloat16),
            jax.ShapeDtypeStruct((rows, width), upstream.dtype),
        ],
        compiler_params=pltpu.CompilerParams(dimension_semantics=("arbitrary",)),
        cost_estimate=pl.CostEstimate(
            flops=flops, transcendentals=rows * width, bytes_accessed=weight.size * 2 + rows * width * 10
        ),
    )(cols, upstream, preact, weight)


def grad_kernel(cols_ref, h_ref, g_ref, out_ref):
    edge = out_ref.shape[-1]
    per_step = out_ref.shape[0]
    step = pl.program_id(0)
    for qq in range(per_step):
        q = step * per_step + qq
        c = cols_ref[q]
        x = h_ref[:, pl.ds(pl.multiple_of(c * edge, edge), edge)]
        j = q // PER_BLOCK
        g = g_ref[:, pl.ds(pl.multiple_of(j * edge, edge), edge)]
        out_ref[qq] = lax.dot_general(
            x, g, (((0,), (0,)), ((), ())), preferred_element_type=jnp.float32
        )


def group_grads(cols, inputs_group, grads_group, pairs, per_step):
    rows, width = inputs_group.shape
    edge = 128
    grid = pltpu.PrefetchScalarGridSpec(
        num_scalar_prefetch=1,
        grid=(pairs // per_step,),
        in_specs=[
            pl.BlockSpec((rows, width), lambda i, c: (0, 0)),
            pl.BlockSpec(grads_group.shape, lambda i, c: (0, 0)),
        ],
        out_specs=pl.BlockSpec((per_step, edge, edge), lambda i, c: (i, 0, 0)),
    )
    return pl.pallas_call(
        grad_kernel,
        grid_spec=grid,
        out_shape=jax.ShapeDtypeStruct((pairs, edge, edge), jnp.float32),
        compiler_params=pltpu.CompilerParams(
            dimension_semantics=("arbitrary",), vmem_limit_bytes=48 * 1024 * 1024
        ),
        cost_estimate=pl.CostEstimate(
            flops=2 * rows * pairs * edge * edge,
            transcendentals=0,
            bytes_accessed=inputs_group.size * 2 + grads_group.size * 2 + pairs * edge * edge * 4,
        ),
    )(cols, inputs_group, grads_group)


def ring_reduce_scatter(chunks, axis, n):
    i = lax.axis_index(axis)
    half = chunks.shape[1] // 2
    east, west = chunks[:, :half], chunks[:, half:]
    cw = [(k, (k + 1) % n) for k in range(n)]
    ccw = [(k, (k - 1) % n) for k in range(n)]
    got_e = got_w = None
    for s in range(n - 1):
        send_e = lax.dynamic_index_in_dim(east, (i - s - 1) % n, 0, False)
        send_w = lax.dynamic_index_in_dim(west, (i + s + 1) % n, 0, False)
        if got_e is not None:
            send_e = got_e + send_e
            send_w = got_w + send_w
        got_e = lax.ppermute(send_e, axis, cw)
        got_w = lax.ppermute(send_w, axis, ccw)
    own_e = lax.dynamic_index_in_dim(east, i, 0, False)
    own_w = lax.dynamic_index_in_dim(west, i, 0, False)
    return jnp.concatenate([got_e + own_e, got_w + own_w], 0)


def body(inputs, cotangent, blocks, block_cols):
    segments = lax.axis_size("segment")
    segment_index = lax.axis_index("segment")
    weight = blocks[0]
    num_blocks, per_block, edge_size = (weight.shape[0], weight.shape[1], weight.shape[2])
    all_rows, layer_width = inputs.shape
    flat_cols = block_cols[0].reshape(-1)

    def hop(block, src, dst):
        return lax.ppermute(block, "segment", [(src, dst)])

    zeros_x = jnp.zeros((all_rows, layer_width), jnp.bfloat16)
    zeros_z = jnp.zeros((all_rows, layer_width), jnp.float32)
    stash_x = inputs
    stash_z = zeros_z
    current = inputs
    for step_now in range(segments):
        active = segment_index == step_now
        held = current
        stash_z, result = lax.cond(
            active,
            lambda: layer_forward(flat_cols, held, weight),
            lambda: (stash_z, zeros_x),
        )
        if step_now > 0:
            stash_x = jnp.where(active, current, stash_x)
        if step_now + 1 < segments:
            current = hop(result, step_now, step_now + 1)
    stash_g = zeros_x
    upstream = cotangent
    for step_now in range(segments):
        owner = segments - 1 - step_now
        active = segment_index == owner
        held = upstream
        stash_g, passed = lax.cond(
            active,
            lambda: layer_backward(flat_cols, held, stash_z, weight),
            lambda: (stash_g, zeros_x),
        )
        if step_now + 1 < segments:
            upstream = hop(passed, owner, owner - 1)
    all_inputs = stash_x
    all_grads = stash_g
    ny, nx, nz = DP_SIZES
    members = ny
    group_pairs = num_blocks * per_block // members
    group_j = num_blocks // members
    member = lax.axis_index("y")
    grads_here = all_grads.reshape(all_rows, members, group_j * edge_size)
    grads_group = lax.all_to_all(
        grads_here, "y", split_axis=1, concat_axis=0, tiled=True
    ).reshape(members * all_rows, group_j * edge_size)
    inputs_group = lax.all_gather(all_inputs, "y", axis=0, tiled=True)
    cols_here = lax.dynamic_slice_in_dim(flat_cols, member * group_pairs, group_pairs)
    partial = group_grads(cols_here, inputs_group, grads_group, group_pairs, 8)
    halves = partial.reshape(nx, group_pairs // nx * edge_size, edge_size)
    side = lax.axis_index("xlo")
    got = lax.ppermute(lax.dynamic_index_in_dim(halves, 1 - side, 0, False), "xlo", [(0, 1), (1, 0)])
    kept = lax.dynamic_index_in_dim(halves, side, 0, False) + got
    own_share = ring_reduce_scatter(kept.reshape(nz, -1, edge_size), "z", nz)
    summed = own_share.astype(jnp.bfloat16)
    return summed[None]


def solution(mesh):
    fine = Mesh(mesh.devices.reshape(mesh.shape["segment"], *DP_SIZES), ("segment",) + DP_AXES)
    return jax.shard_map(
        body,
        mesh=fine,
        in_specs=(
            P(DP_AXES, None),
            P(DP_AXES, None),
            P("segment", None, None, None, None),
            P("segment", None, None),
        ),
        out_specs=P("segment", DP_AXES, None),
        check_vma=False,
    )
```

```python
import functools

import jax
import jax.numpy as jnp
import numpy as np
from jax import lax
from jax.experimental import pallas as pl
from jax.experimental.pallas import tpu as pltpu
from jax.sharding import Mesh, PartitionSpec as P

DP_AXES = ("y", "xlo", "z")
DP_SIZES = (4, 2, 8)
JB = 8
PER_BLOCK = 8


def from_behind(block, axis, distance):
    devices = range(lax.axis_size(axis))
    route = [(i - distance, i) for i in devices if i - distance in devices]
    return lax.ppermute(block, axis, route)


def forward_kernel(cols_ref, h_ref, w_ref, z_ref, out_ref):
    edge = w_ref.shape[-1]
    per_block = w_ref.shape[1]
    step = pl.program_id(0)
    for jj in range(w_ref.shape[0]):
        j = step * w_ref.shape[0] + jj
        picked = jnp.concatenate(
            [
                h_ref[:, pl.ds(pl.multiple_of(cols_ref[j * per_block + k] * edge, edge), edge)]
                for k in range(per_block)
            ],
            axis=1,
        )
        acc = jnp.dot(
            picked, w_ref[jj].reshape(per_block * edge, edge), preferred_element_type=jnp.float32
        )
        z_ref[:, jj * edge:(jj + 1) * edge] = acc
        own = h_ref[:, pl.ds(pl.multiple_of(j * edge, edge), edge)].astype(jnp.float32)
        out_ref[:, jj * edge:(jj + 1) * edge] = (own + acc * jax.nn.sigmoid(acc)).astype(out_ref.dtype)


def backward_kernel(cols_ref, up_ref, z_ref, w_ref, g_ref, new_ref, back_ref):
    edge = w_ref.shape[-1]
    per_block = w_ref.shape[1]
    step = pl.program_id(0)

    @pl.when(step == 0)
    def _():
        back_ref[...] = jnp.zeros_like(back_ref)

    for jj in range(w_ref.shape[0]):
        j = step * w_ref.shape[0] + jj
        z = z_ref[:, jj * edge:(jj + 1) * edge]
        u = up_ref[:, pl.ds(pl.multiple_of(j * edge, edge), edge)].astype(jnp.float32)
        s = jax.nn.sigmoid(z)
        g = (u * s * (1.0 + z * (1.0 - s))).astype(jnp.bfloat16)
        g_ref[:, jj * edge:(jj + 1) * edge] = g
        spread = lax.dot_general(
            g,
            w_ref[jj].reshape(per_block * edge, edge),
            (((1,), (1,)), ((), ())),
            preferred_element_type=jnp.float32,
        )
        for k in range(per_block):
            c = cols_ref[j * per_block + k]
            at = pl.ds(pl.multiple_of(c * edge, edge), edge)
            back_ref[:, at] = back_ref[:, at] + spread[:, k * edge:(k + 1) * edge]

    @pl.when(step == pl.num_programs(0) - 1)
    def _():
        new_ref[...] = (up_ref[...].astype(jnp.float32) + back_ref[...]).astype(new_ref.dtype)


def layer_forward(cols, hidden, weight):
    rows, width = hidden.shape
    num_blocks, per_block, edge, _ = weight.shape
    grid = pltpu.PrefetchScalarGridSpec(
        num_scalar_prefetch=1,
        grid=(num_blocks // JB,),
        in_specs=[
            pl.BlockSpec((rows, width), lambda i, c: (0, 0)),
            pl.BlockSpec((JB, per_block, edge, edge), lambda i, c: (i, 0, 0, 0)),
        ],
        out_specs=[
            pl.BlockSpec((rows, JB * edge), lambda i, c: (0, i)),
            pl.BlockSpec((rows, JB * edge), lambda i, c: (0, i)),
        ],
    )
    flops = 2 * rows * num_blocks * per_block * edge * edge
    return pl.pallas_call(
        forward_kernel,
        grid_spec=grid,
        out_shape=[
            jax.ShapeDtypeStruct((rows, width), jnp.float32),
            jax.ShapeDtypeStruct((rows, width), hidden.dtype),
        ],
        compiler_params=pltpu.CompilerParams(dimension_semantics=("arbitrary",)),
        cost_estimate=pl.CostEstimate(
            flops=flops, transcendentals=rows * width, bytes_accessed=weight.size * 2 + rows * width * 8
        ),
    )(cols, hidden, weight)


def layer_backward(cols, upstream, preact, weight):
    rows, width = upstream.shape
    num_blocks, per_block, edge, _ = weight.shape
    grid = pltpu.PrefetchScalarGridSpec(
        num_scalar_prefetch=1,
        grid=(num_blocks // JB,),
        in_specs=[
            pl.BlockSpec((rows, width), lambda i, c: (0, 0)),
            pl.BlockSpec((rows, JB * edge), lambda i, c: (0, i)),
            pl.BlockSpec((JB, per_block, edge, edge), lambda i, c: (i, 0, 0, 0)),
        ],
        out_specs=[
            pl.BlockSpec((rows, JB * edge), lambda i, c: (0, i)),
            pl.BlockSpec((rows, width), lambda i, c: (0, 0)),
        ],
        scratch_shapes=[pltpu.VMEM((rows, width), jnp.float32)],
    )
    flops = 2 * rows * num_blocks * per_block * edge * edge
    return pl.pallas_call(
        backward_kernel,
        grid_spec=grid,
        out_shape=[
            jax.ShapeDtypeStruct((rows, width), jnp.bfloat16),
            jax.ShapeDtypeStruct((rows, width), upstream.dtype),
        ],
        compiler_params=pltpu.CompilerParams(dimension_semantics=("arbitrary",)),
        cost_estimate=pl.CostEstimate(
            flops=flops, transcendentals=rows * width, bytes_accessed=weight.size * 2 + rows * width * 10
        ),
    )(cols, upstream, preact, weight)


def grad_kernel(cols_ref, j_ref, h_ref, g_ref, out_ref):
    edge = out_ref.shape[-1]
    per_step = out_ref.shape[0]
    step = pl.program_id(0)
    for qq in range(per_step):
        q = step * per_step + qq
        c = cols_ref[q]
        x = h_ref[:, pl.ds(pl.multiple_of(c * edge, edge), edge)]
        j = j_ref[q]
        g = g_ref[:, pl.ds(pl.multiple_of(j * edge, edge), edge)]
        out_ref[qq] = lax.dot_general(
            x, g, (((0,), (0,)), ((), ())), preferred_element_type=jnp.float32
        )


def group_grads(cols, j_index, inputs_group, grads_group, pairs, per_step):
    rows, width = inputs_group.shape
    edge = 128
    grid = pltpu.PrefetchScalarGridSpec(
        num_scalar_prefetch=2,
        grid=(pairs // per_step,),
        in_specs=[
            pl.BlockSpec((rows, width), lambda i, c, j: (0, 0)),
            pl.BlockSpec(grads_group.shape, lambda i, c, j: (0, 0)),
        ],
        out_specs=pl.BlockSpec((per_step, edge, edge), lambda i, c, j: (i, 0, 0)),
    )
    return pl.pallas_call(
        grad_kernel,
        grid_spec=grid,
        out_shape=jax.ShapeDtypeStruct((pairs, edge, edge), jnp.float32),
        compiler_params=pltpu.CompilerParams(
            dimension_semantics=("arbitrary",), vmem_limit_bytes=48 * 1024 * 1024
        ),
        cost_estimate=pl.CostEstimate(
            flops=2 * rows * pairs * edge * edge,
            transcendentals=0,
            bytes_accessed=inputs_group.size * 2 + grads_group.size * 2 + pairs * edge * edge * 4,
        ),
    )(cols, j_index, inputs_group, grads_group)


def ring_reduce_scatter(chunks, axis, n):
    i = lax.axis_index(axis)
    half = chunks.shape[1] // 2
    east, west = chunks[:, :half], chunks[:, half:]
    cw = [(k, (k + 1) % n) for k in range(n)]
    ccw = [(k, (k - 1) % n) for k in range(n)]
    got_e = got_w = None
    for s in range(n - 1):
        send_e = lax.dynamic_index_in_dim(east, (i - s - 1) % n, 0, False)
        send_w = lax.dynamic_index_in_dim(west, (i + s + 1) % n, 0, False)
        if got_e is not None:
            send_e = got_e + send_e
            send_w = got_w + send_w
        got_e = lax.ppermute(send_e, axis, cw)
        got_w = lax.ppermute(send_w, axis, ccw)
    own_e = lax.dynamic_index_in_dim(east, i, 0, False)
    own_w = lax.dynamic_index_in_dim(west, i, 0, False)
    return jnp.concatenate([got_e + own_e, got_w + own_w], 0)


def body(inputs, cotangent, blocks, block_cols):
    segments = lax.axis_size("segment")
    segment_index = lax.axis_index("segment")
    weight = blocks[0]
    num_blocks, per_block, edge_size = (weight.shape[0], weight.shape[1], weight.shape[2])
    all_rows, layer_width = inputs.shape
    flat_cols = block_cols[0].reshape(-1)

    def hop(block, src, dst):
        return lax.ppermute(block, "segment", [(src, dst)])

    zeros_x = jnp.zeros((all_rows, layer_width), jnp.bfloat16)
    zeros_z = jnp.zeros((all_rows, layer_width), jnp.float32)
    stash_x = inputs
    stash_z = zeros_z
    current = inputs
    for step_now in range(segments):
        active = segment_index == step_now
        held = current
        stash_z, result = lax.cond(
            active,
            lambda: layer_forward(flat_cols, held, weight),
            lambda: (stash_z, zeros_x),
        )
        if step_now > 0:
            stash_x = jnp.where(active, current, stash_x)
        if step_now + 1 < segments:
            current = hop(result, step_now, step_now + 1)
    stash_g = zeros_x
    upstream = cotangent
    for step_now in range(segments):
        owner = segments - 1 - step_now
        active = segment_index == owner
        held = upstream
        stash_g, passed = lax.cond(
            active,
            lambda: layer_backward(flat_cols, held, stash_z, weight),
            lambda: (stash_g, zeros_x),
        )
        if step_now + 1 < segments:
            upstream = hop(passed, owner, owner - 1)
    all_inputs = stash_x
    all_grads = stash_g
    ny, nx, nz = DP_SIZES
    members = ny
    group_pairs = num_blocks * per_block // members
    group_j = num_blocks // members
    member = lax.axis_index("y")
    grads_here = all_grads.reshape(all_rows, members, group_j * edge_size)
    grads_group = lax.all_to_all(
        grads_here, "y", split_axis=1, concat_axis=0, tiled=True
    ).reshape(members * all_rows, group_j * edge_size)
    inputs_group = lax.all_gather(all_inputs, "y", axis=0, tiled=True)
    cols_here = lax.dynamic_slice_in_dim(flat_cols, member * group_pairs, group_pairs)
    order = np.arange(group_pairs).reshape(nx, nz, -1).transpose(1, 0, 2).reshape(-1)
    j_index = jnp.asarray(order // per_block, jnp.int32)
    partial = group_grads(cols_here[order], j_index, inputs_group, grads_group, group_pairs, 8)
    reduced = ring_reduce_scatter(partial.reshape(nz, -1, edge_size), "z", nz)
    halves = reduced.reshape(nx, -1, edge_size)
    side = lax.axis_index("xlo")
    got = lax.ppermute(lax.dynamic_index_in_dim(halves, 1 - side, 0, False), "xlo", [(0, 1), (1, 0)])
    own_share = lax.dynamic_index_in_dim(halves, side, 0, False) + got
    summed = own_share.astype(jnp.bfloat16)
    return summed[None]


def solution(mesh):
    fine = Mesh(mesh.devices.reshape(mesh.shape["segment"], *DP_SIZES), ("segment",) + DP_AXES)
    return jax.shard_map(
        body,
        mesh=fine,
        in_specs=(
            P(DP_AXES, None),
            P(DP_AXES, None),
            P("segment", None, None, None, None),
            P("segment", None, None),
        ),
        out_specs=P("segment", DP_AXES, None),
        check_vma=False,
    )
```

```python
import functools

import jax
import jax.numpy as jnp
import numpy as np
from jax import lax
from jax.experimental import pallas as pl
from jax.experimental.pallas import tpu as pltpu
from jax.sharding import Mesh, PartitionSpec as P

DP_AXES = ("y", "xlo", "z")
DP_SIZES = (4, 2, 8)
JB = 8
PER_BLOCK = 8


def from_behind(block, axis, distance):
    devices = range(lax.axis_size(axis))
    route = [(i - distance, i) for i in devices if i - distance in devices]
    return lax.ppermute(block, axis, route)


def forward_kernel(first, cols_ref, h_ref, w_ref, z_ref, out_ref):
    edge = w_ref.shape[-1]
    per_block = w_ref.shape[1]
    step = first + pl.program_id(0)
    for jj in range(w_ref.shape[0]):
        j = step * w_ref.shape[0] + jj
        picked = jnp.concatenate(
            [
                h_ref[:, pl.ds(pl.multiple_of(cols_ref[j * per_block + k] * edge, edge), edge)]
                for k in range(per_block)
            ],
            axis=1,
        )
        acc = jnp.dot(
            picked, w_ref[jj].reshape(per_block * edge, edge), preferred_element_type=jnp.float32
        )
        z_ref[:, jj * edge:(jj + 1) * edge] = acc
        own = h_ref[:, pl.ds(pl.multiple_of(j * edge, edge), edge)].astype(jnp.float32)
        out_ref[:, jj * edge:(jj + 1) * edge] = (own + acc * jax.nn.sigmoid(acc)).astype(out_ref.dtype)


def backward_kernel(cols_ref, up_ref, z_ref, w_ref, g_ref, new_ref, back_ref):
    edge = w_ref.shape[-1]
    per_block = w_ref.shape[1]
    step = pl.program_id(0)

    @pl.when(step == 0)
    def _():
        back_ref[...] = jnp.zeros_like(back_ref)

    for jj in range(w_ref.shape[0]):
        j = step * w_ref.shape[0] + jj
        z = z_ref[:, jj * edge:(jj + 1) * edge]
        u = up_ref[:, pl.ds(pl.multiple_of(j * edge, edge), edge)].astype(jnp.float32)
        s = jax.nn.sigmoid(z)
        g = (u * s * (1.0 + z * (1.0 - s))).astype(jnp.bfloat16)
        g_ref[:, jj * edge:(jj + 1) * edge] = g
        spread = lax.dot_general(
            g,
            w_ref[jj].reshape(per_block * edge, edge),
            (((1,), (1,)), ((), ())),
            preferred_element_type=jnp.float32,
        )
        for k in range(per_block):
            c = cols_ref[j * per_block + k]
            at = pl.ds(pl.multiple_of(c * edge, edge), edge)
            back_ref[:, at] = back_ref[:, at] + spread[:, k * edge:(k + 1) * edge]

    @pl.when(step == pl.num_programs(0) - 1)
    def _():
        new_ref[...] = (up_ref[...].astype(jnp.float32) + back_ref[...]).astype(new_ref.dtype)


def layer_forward(cols, hidden, weight, first, count):
    rows, width = hidden.shape
    num_blocks, per_block, edge, _ = weight.shape
    grid = pltpu.PrefetchScalarGridSpec(
        num_scalar_prefetch=1,
        grid=(count,),
        in_specs=[
            pl.BlockSpec((rows, width), lambda i, c: (0, 0)),
            pl.BlockSpec((JB, per_block, edge, edge), lambda i, c: (first + i, 0, 0, 0)),
        ],
        out_specs=[
            pl.BlockSpec((rows, JB * edge), lambda i, c: (0, i)),
            pl.BlockSpec((rows, JB * edge), lambda i, c: (0, i)),
        ],
    )
    flops = 2 * rows * count * JB * per_block * edge * edge
    out_width = count * JB * edge
    return pl.pallas_call(
        functools.partial(forward_kernel, first),
        grid_spec=grid,
        out_shape=[
            jax.ShapeDtypeStruct((rows, out_width), jnp.float32),
            jax.ShapeDtypeStruct((rows, out_width), hidden.dtype),
        ],
        compiler_params=pltpu.CompilerParams(dimension_semantics=("arbitrary",)),
        cost_estimate=pl.CostEstimate(
            flops=flops,
            transcendentals=rows * out_width,
            bytes_accessed=count * JB * per_block * edge * edge * 2 + rows * width * 2 + rows * out_width * 6,
        ),
    )(cols, hidden, weight)


def layer_backward(cols, upstream, preact, weight):
    rows, width = upstream.shape
    num_blocks, per_block, edge, _ = weight.shape
    grid = pltpu.PrefetchScalarGridSpec(
        num_scalar_prefetch=1,
        grid=(num_blocks // JB,),
        in_specs=[
            pl.BlockSpec((rows, width), lambda i, c: (0, 0)),
            pl.BlockSpec((rows, JB * edge), lambda i, c: (0, i)),
            pl.BlockSpec((JB, per_block, edge, edge), lambda i, c: (i, 0, 0, 0)),
        ],
        out_specs=[
            pl.BlockSpec((rows, JB * edge), lambda i, c: (0, i)),
            pl.BlockSpec((rows, width), lambda i, c: (0, 0)),
        ],
        scratch_shapes=[pltpu.VMEM((rows, width), jnp.float32)],
    )
    flops = 2 * rows * num_blocks * per_block * edge * edge
    return pl.pallas_call(
        backward_kernel,
        grid_spec=grid,
        out_shape=[
            jax.ShapeDtypeStruct((rows, width), jnp.bfloat16),
            jax.ShapeDtypeStruct((rows, width), upstream.dtype),
        ],
        compiler_params=pltpu.CompilerParams(dimension_semantics=("arbitrary",)),
        cost_estimate=pl.CostEstimate(
            flops=flops, transcendentals=rows * width, bytes_accessed=weight.size * 2 + rows * width * 10
        ),
    )(cols, upstream, preact, weight)


def grad_kernel(cols_ref, j_ref, h_ref, g_ref, out_ref):
    edge = out_ref.shape[-1]
    per_step = out_ref.shape[0]
    step = pl.program_id(0)
    for qq in range(per_step):
        q = step * per_step + qq
        c = cols_ref[q]
        x = h_ref[:, pl.ds(pl.multiple_of(c * edge, edge), edge)]
        j = j_ref[q]
        g = g_ref[:, pl.ds(pl.multiple_of(j * edge, edge), edge)]
        out_ref[qq] = lax.dot_general(
            x, g, (((0,), (0,)), ((), ())), preferred_element_type=jnp.float32
        )


def group_grads(cols, j_index, inputs_group, grads_group, pairs, per_step):
    rows, width = inputs_group.shape
    edge = 128
    grid = pltpu.PrefetchScalarGridSpec(
        num_scalar_prefetch=2,
        grid=(pairs // per_step,),
        in_specs=[
            pl.BlockSpec((rows, width), lambda i, c, j: (0, 0)),
            pl.BlockSpec(grads_group.shape, lambda i, c, j: (0, 0)),
        ],
        out_specs=pl.BlockSpec((per_step, edge, edge), lambda i, c, j: (i, 0, 0)),
    )
    return pl.pallas_call(
        grad_kernel,
        grid_spec=grid,
        out_shape=jax.ShapeDtypeStruct((pairs, edge, edge), jnp.float32),
        compiler_params=pltpu.CompilerParams(
            dimension_semantics=("arbitrary",), vmem_limit_bytes=48 * 1024 * 1024
        ),
        cost_estimate=pl.CostEstimate(
            flops=2 * rows * pairs * edge * edge,
            transcendentals=0,
            bytes_accessed=inputs_group.size * 2 + grads_group.size * 2 + pairs * edge * edge * 4,
        ),
    )(cols, j_index, inputs_group, grads_group)


def ring_reduce_scatter(chunks, axis, n):
    i = lax.axis_index(axis)
    half = chunks.shape[1] // 2
    east, west = chunks[:, :half], chunks[:, half:]
    cw = [(k, (k + 1) % n) for k in range(n)]
    ccw = [(k, (k - 1) % n) for k in range(n)]
    got_e = got_w = None
    for s in range(n - 1):
        send_e = lax.dynamic_index_in_dim(east, (i - s - 1) % n, 0, False)
        send_w = lax.dynamic_index_in_dim(west, (i + s + 1) % n, 0, False)
        if got_e is not None:
            send_e = got_e + send_e
            send_w = got_w + send_w
        got_e = lax.ppermute(send_e, axis, cw)
        got_w = lax.ppermute(send_w, axis, ccw)
    own_e = lax.dynamic_index_in_dim(east, i, 0, False)
    own_w = lax.dynamic_index_in_dim(west, i, 0, False)
    return jnp.concatenate([got_e + own_e, got_w + own_w], 0)


def body(inputs, cotangent, blocks, block_cols):
    segments = lax.axis_size("segment")
    segment_index = lax.axis_index("segment")
    weight = blocks[0]
    num_blocks, per_block, edge_size = (weight.shape[0], weight.shape[1], weight.shape[2])
    all_rows, layer_width = inputs.shape
    flat_cols = block_cols[0].reshape(-1)

    def hop(block, src, dst):
        return lax.ppermute(block, "segment", [(src, dst)])

    zeros_x = jnp.zeros((all_rows, layer_width), jnp.bfloat16)
    halves = num_blocks // JB // 2
    zeros_half = jnp.zeros((all_rows, layer_width // 2), jnp.bfloat16)
    stash_halves = [jnp.zeros((all_rows, layer_width // 2), jnp.float32)] * 2
    stash_x = inputs
    current = inputs
    for step_now in range(segments):
        active = segment_index == step_now
        held = current
        sent = []
        for part in range(2):
            kept = stash_halves[part]
            stash_halves[part], result = lax.cond(
                active,
                lambda part=part: layer_forward(flat_cols, held, weight, part * halves, halves),
                lambda kept=kept: (kept, zeros_half),
            )
            if step_now + 1 < segments:
                sent.append(hop(result, step_now, step_now + 1))
        if step_now > 0:
            stash_x = jnp.where(active, current, stash_x)
        if sent:
            current = jnp.concatenate(sent, axis=1)
    stash_z = jnp.concatenate(stash_halves, axis=1)
    stash_g = zeros_x
    upstream = cotangent
    for step_now in range(segments):
        owner = segments - 1 - step_now
        active = segment_index == owner
        held = upstream
        stash_g, passed = lax.cond(
            active,
            lambda: layer_backward(flat_cols, held, stash_z, weight),
            lambda: (stash_g, zeros_x),
        )
        if step_now + 1 < segments:
            upstream = hop(passed, owner, owner - 1)
    all_inputs = stash_x
    all_grads = stash_g
    ny, nx, nz = DP_SIZES
    members = ny
    group_pairs = num_blocks * per_block // members
    group_j = num_blocks // members
    member = lax.axis_index("y")
    grads_here = all_grads.reshape(all_rows, members, group_j * edge_size)
    grads_group = lax.all_to_all(
        grads_here, "y", split_axis=1, concat_axis=0, tiled=True
    ).reshape(members * all_rows, group_j * edge_size)
    inputs_group = lax.all_gather(all_inputs, "y", axis=0, tiled=True)
    cols_here = lax.dynamic_slice_in_dim(flat_cols, member * group_pairs, group_pairs)
    order = np.arange(group_pairs).reshape(nx, nz, -1).transpose(1, 0, 2).reshape(-1)
    j_index = jnp.asarray(order // per_block, jnp.int32)
    partial = group_grads(cols_here[order], j_index, inputs_group, grads_group, group_pairs, 8)
    reduced = ring_reduce_scatter(partial.reshape(nz, -1, edge_size), "z", nz)
    halves = reduced.reshape(nx, -1, edge_size)
    side = lax.axis_index("xlo")
    got = lax.ppermute(lax.dynamic_index_in_dim(halves, 1 - side, 0, False), "xlo", [(0, 1), (1, 0)])
    own_share = lax.dynamic_index_in_dim(halves, side, 0, False) + got
    summed = own_share.astype(jnp.bfloat16)
    return summed[None]


def solution(mesh):
    fine = Mesh(mesh.devices.reshape(mesh.shape["segment"], *DP_SIZES), ("segment",) + DP_AXES)
    return jax.shard_map(
        body,
        mesh=fine,
        in_specs=(
            P(DP_AXES, None),
            P(DP_AXES, None),
            P("segment", None, None, None, None),
            P("segment", None, None),
        ),
        out_specs=P("segment", DP_AXES, None),
        check_vma=False,
    )
```

```python
import functools

import jax
import jax.numpy as jnp
import numpy as np
from jax import lax
from jax.experimental import pallas as pl
from jax.experimental.pallas import tpu as pltpu
from jax.sharding import Mesh, PartitionSpec as P

DP_AXES = ("y", "xlo", "z")
DP_SIZES = (4, 2, 8)
JB = 8
PER_BLOCK = 8


def from_behind(block, axis, distance):
    devices = range(lax.axis_size(axis))
    route = [(i - distance, i) for i in devices if i - distance in devices]
    return lax.ppermute(block, axis, route)


def forward_kernel(cols_ref, h_ref, w_ref, z_ref, out_ref):
    edge = w_ref.shape[-1]
    per_block = w_ref.shape[1]
    step = pl.program_id(0)
    for jj in range(w_ref.shape[0]):
        j = step * w_ref.shape[0] + jj
        picked = jnp.concatenate(
            [
                h_ref[:, pl.ds(pl.multiple_of(cols_ref[j * per_block + k] * edge, edge), edge)]
                for k in range(per_block)
            ],
            axis=1,
        )
        acc = jnp.dot(
            picked, w_ref[jj].reshape(per_block * edge, edge), preferred_element_type=jnp.float32
        )
        z_ref[:, jj * edge:(jj + 1) * edge] = acc
        own = h_ref[:, pl.ds(pl.multiple_of(j * edge, edge), edge)].astype(jnp.float32)
        out_ref[:, jj * edge:(jj + 1) * edge] = (own + acc * jax.nn.sigmoid(acc)).astype(out_ref.dtype)


def backward_kernel(cols_ref, up_ref, z_ref, w_ref, g_ref, new_ref, back_ref):
    edge = w_ref.shape[-1]
    per_block = w_ref.shape[1]
    step = pl.program_id(0)

    @pl.when(step == 0)
    def _():
        back_ref[...] = jnp.zeros_like(back_ref)

    for jj in range(w_ref.shape[0]):
        j = step * w_ref.shape[0] + jj
        z = z_ref[:, jj * edge:(jj + 1) * edge]
        u = up_ref[:, pl.ds(pl.multiple_of(j * edge, edge), edge)].astype(jnp.float32)
        s = jax.nn.sigmoid(z)
        g = (u * s * (1.0 + z * (1.0 - s))).astype(jnp.bfloat16)
        g_ref[:, jj * edge:(jj + 1) * edge] = g
        spread = lax.dot_general(
            g,
            w_ref[jj].reshape(per_block * edge, edge),
            (((1,), (1,)), ((), ())),
            preferred_element_type=jnp.float32,
        )
        for k in range(per_block):
            c = cols_ref[j * per_block + k]
            at = pl.ds(pl.multiple_of(c * edge, edge), edge)
            back_ref[:, at] = back_ref[:, at] + spread[:, k * edge:(k + 1) * edge]

    @pl.when(step == pl.num_programs(0) - 1)
    def _():
        new_ref[...] = (up_ref[...].astype(jnp.float32) + back_ref[...]).astype(new_ref.dtype)


def layer_forward(cols, hidden, weight):
    rows, width = hidden.shape
    num_blocks, per_block, edge, _ = weight.shape
    grid = pltpu.PrefetchScalarGridSpec(
        num_scalar_prefetch=1,
        grid=(num_blocks // JB,),
        in_specs=[
            pl.BlockSpec((rows, width), lambda i, c: (0, 0)),
            pl.BlockSpec((JB, per_block, edge, edge), lambda i, c: (i, 0, 0, 0)),
        ],
        out_specs=[
            pl.BlockSpec((rows, JB * edge), lambda i, c: (0, i)),
            pl.BlockSpec((rows, JB * edge), lambda i, c: (0, i)),
        ],
    )
    flops = 2 * rows * num_blocks * per_block * edge * edge
    return pl.pallas_call(
        forward_kernel,
        grid_spec=grid,
        out_shape=[
            jax.ShapeDtypeStruct((rows, width), jnp.float32),
            jax.ShapeDtypeStruct((rows, width), hidden.dtype),
        ],
        compiler_params=pltpu.CompilerParams(dimension_semantics=("arbitrary",)),
        cost_estimate=pl.CostEstimate(
            flops=flops, transcendentals=rows * width, bytes_accessed=weight.size * 2 + rows * width * 8
        ),
    )(cols, hidden, weight)


def layer_backward(cols, upstream, preact, weight):
    rows, width = upstream.shape
    num_blocks, per_block, edge, _ = weight.shape
    grid = pltpu.PrefetchScalarGridSpec(
        num_scalar_prefetch=1,
        grid=(num_blocks // JB,),
        in_specs=[
            pl.BlockSpec((rows, width), lambda i, c: (0, 0)),
            pl.BlockSpec((rows, JB * edge), lambda i, c: (0, i)),
            pl.BlockSpec((JB, per_block, edge, edge), lambda i, c: (i, 0, 0, 0)),
        ],
        out_specs=[
            pl.BlockSpec((rows, JB * edge), lambda i, c: (0, i)),
            pl.BlockSpec((rows, width), lambda i, c: (0, 0)),
        ],
        scratch_shapes=[pltpu.VMEM((rows, width), jnp.float32)],
    )
    flops = 2 * rows * num_blocks * per_block * edge * edge
    return pl.pallas_call(
        backward_kernel,
        grid_spec=grid,
        out_shape=[
            jax.ShapeDtypeStruct((rows, width), jnp.bfloat16),
            jax.ShapeDtypeStruct((rows, width), upstream.dtype),
        ],
        compiler_params=pltpu.CompilerParams(dimension_semantics=("arbitrary",)),
        cost_estimate=pl.CostEstimate(
            flops=flops, transcendentals=rows * width, bytes_accessed=weight.size * 2 + rows * width * 10
        ),
    )(cols, upstream, preact, weight)


def grad_kernel(cols_ref, j_ref, h_ref, g_ref, out_ref):
    edge = out_ref.shape[-1]
    per_step = out_ref.shape[0]
    step = pl.program_id(0)
    for qq in range(per_step):
        q = step * per_step + qq
        c = cols_ref[q]
        x = h_ref[:, pl.ds(pl.multiple_of(c * edge, edge), edge)]
        j = j_ref[q]
        g = g_ref[:, pl.ds(pl.multiple_of(j * edge, edge), edge)]
        out_ref[qq] = lax.dot_general(
            x, g, (((0,), (0,)), ((), ())), preferred_element_type=jnp.float32
        )


def group_grads(cols, j_index, inputs_group, grads_group, pairs, per_step):
    rows, width = inputs_group.shape
    edge = 128
    grid = pltpu.PrefetchScalarGridSpec(
        num_scalar_prefetch=2,
        grid=(pairs // per_step,),
        in_specs=[
            pl.BlockSpec((rows, width), lambda i, c, j: (0, 0)),
            pl.BlockSpec(grads_group.shape, lambda i, c, j: (0, 0)),
        ],
        out_specs=pl.BlockSpec((per_step, edge, edge), lambda i, c, j: (i, 0, 0)),
    )
    return pl.pallas_call(
        grad_kernel,
        grid_spec=grid,
        out_shape=jax.ShapeDtypeStruct((pairs, edge, edge), jnp.float32),
        compiler_params=pltpu.CompilerParams(
            dimension_semantics=("arbitrary",), vmem_limit_bytes=48 * 1024 * 1024
        ),
        cost_estimate=pl.CostEstimate(
            flops=2 * rows * pairs * edge * edge,
            transcendentals=0,
            bytes_accessed=inputs_group.size * 2 + grads_group.size * 2 + pairs * edge * edge * 4,
        ),
    )(cols, j_index, inputs_group, grads_group)


def ring_reduce_scatter(chunks, axis, n):
    i = lax.axis_index(axis)
    half = chunks.shape[1] // 2
    east, west = chunks[:, :half], chunks[:, half:]
    cw = [(k, (k + 1) % n) for k in range(n)]
    ccw = [(k, (k - 1) % n) for k in range(n)]
    got_e = got_w = None
    for s in range(n - 1):
        send_e = lax.dynamic_index_in_dim(east, (i - s - 1) % n, 0, False)
        send_w = lax.dynamic_index_in_dim(west, (i + s + 1) % n, 0, False)
        if got_e is not None:
            send_e = got_e + send_e
            send_w = got_w + send_w
        got_e = lax.ppermute(send_e, axis, cw)
        got_w = lax.ppermute(send_w, axis, ccw)
    own_e = lax.dynamic_index_in_dim(east, i, 0, False)
    own_w = lax.dynamic_index_in_dim(west, i, 0, False)
    return jnp.concatenate([got_e + own_e, got_w + own_w], 0)


def body(inputs, cotangent, blocks, block_cols):
    segments = lax.axis_size("segment")
    segment_index = lax.axis_index("segment")
    weight = blocks[0]
    num_blocks, per_block, edge_size = (weight.shape[0], weight.shape[1], weight.shape[2])
    all_rows, layer_width = inputs.shape
    flat_cols = block_cols[0].reshape(-1)

    def hop(block, src, dst):
        return lax.ppermute(block, "segment", [(src, dst)])

    zeros_x = jnp.zeros((all_rows, layer_width), jnp.bfloat16)
    zeros_z = jnp.zeros((all_rows, layer_width), jnp.float32)
    stash_x = inputs
    stash_z = zeros_z
    current = inputs
    for step_now in range(segments):
        active = segment_index == step_now
        held = current
        stash_z, result = lax.cond(
            active,
            lambda: layer_forward(flat_cols, held, weight),
            lambda: (stash_z, zeros_x),
        )
        if step_now > 0:
            stash_x = jnp.where(active, current, stash_x)
        if step_now + 1 < segments:
            current = hop(result, step_now, step_now + 1)
    stash_g = zeros_x
    upstream = cotangent
    for step_now in range(segments):
        owner = segments - 1 - step_now
        active = segment_index == owner
        held = upstream
        stash_g, passed = lax.cond(
            active,
            lambda: layer_backward(flat_cols, held, stash_z, weight),
            lambda: (stash_g, zeros_x),
        )
        if step_now + 1 < segments:
            upstream = hop(passed, owner, owner - 1)
    all_inputs = stash_x
    all_grads = stash_g
    ny, nx, nz = DP_SIZES
    members = ny
    group_pairs = num_blocks * per_block // members
    group_j = num_blocks // members
    member = lax.axis_index("y")
    grads_here = all_grads.reshape(all_rows, members, group_j * edge_size)
    pieces = [lax.dynamic_index_in_dim(grads_here, member, 1, False)]
    for offset in range(1, members):
        route = [(i, (i + offset) % members) for i in range(members)]
        outgoing = lax.dynamic_index_in_dim(grads_here, (member + offset) % members, 1, False)
        pieces.append(lax.ppermute(outgoing, "y", route))
    by_offset = jnp.stack(pieces)
    sender_offset = (member - jnp.arange(members, dtype=jnp.int32)) % members
    grads_group = jnp.take(by_offset, sender_offset, axis=0).reshape(
        members * all_rows, group_j * edge_size
    )
    inputs_group = lax.all_gather(all_inputs, "y", axis=0, tiled=True)
    cols_here = lax.dynamic_slice_in_dim(flat_cols, member * group_pairs, group_pairs)
    order = np.arange(group_pairs).reshape(nx, nz, -1).transpose(1, 0, 2).reshape(-1)
    j_index = jnp.asarray(order // per_block, jnp.int32)
    partial = group_grads(cols_here[order], j_index, inputs_group, grads_group, group_pairs, 16)
    reduced = ring_reduce_scatter(partial.reshape(nz, -1, edge_size), "z", nz)
    halves = reduced.reshape(nx, -1, edge_size)
    side = lax.axis_index("xlo")
    got = lax.ppermute(lax.dynamic_index_in_dim(halves, 1 - side, 0, False), "xlo", [(0, 1), (1, 0)])
    own_share = lax.dynamic_index_in_dim(halves, side, 0, False) + got
    summed = own_share.astype(jnp.bfloat16)
    return summed[None]


def solution(mesh):
    fine = Mesh(mesh.devices.reshape(mesh.shape["segment"], *DP_SIZES), ("segment",) + DP_AXES)
    return jax.shard_map(
        body,
        mesh=fine,
        in_specs=(
            P(DP_AXES, None),
            P(DP_AXES, None),
            P("segment", None, None, None, None),
            P("segment", None, None),
        ),
        out_specs=P("segment", DP_AXES, None),
        check_vma=False,
    )
```

```python
import functools

import jax
import jax.numpy as jnp
import numpy as np
from jax import lax
from jax.experimental import pallas as pl
from jax.experimental.pallas import tpu as pltpu
from jax.sharding import Mesh, PartitionSpec as P

DP_AXES = ("y", "xlo", "z")
DP_SIZES = (4, 2, 8)
JB = 8
PER_BLOCK = 8


def from_behind(block, axis, distance):
    devices = range(lax.axis_size(axis))
    route = [(i - distance, i) for i in devices if i - distance in devices]
    return lax.ppermute(block, axis, route)


def forward_kernel(cols_ref, h_ref, w_ref, z_ref, out_ref):
    edge = w_ref.shape[-1]
    per_block = w_ref.shape[1]
    step = pl.program_id(0)
    for jj in range(w_ref.shape[0]):
        j = step * w_ref.shape[0] + jj
        picked = jnp.concatenate(
            [
                h_ref[:, pl.ds(pl.multiple_of(cols_ref[j * per_block + k] * edge, edge), edge)]
                for k in range(per_block)
            ],
            axis=1,
        )
        acc = jnp.dot(
            picked, w_ref[jj].reshape(per_block * edge, edge), preferred_element_type=jnp.float32
        )
        z_ref[:, jj * edge:(jj + 1) * edge] = acc
        own = h_ref[:, pl.ds(pl.multiple_of(j * edge, edge), edge)].astype(jnp.float32)
        out_ref[:, jj * edge:(jj + 1) * edge] = (own + acc * jax.nn.sigmoid(acc)).astype(out_ref.dtype)


def backward_kernel(cols_ref, up_ref, z_ref, w_ref, g_ref, new_ref, back_ref):
    edge = w_ref.shape[-1]
    per_block = w_ref.shape[1]
    step = pl.program_id(0)

    @pl.when(step == 0)
    def _():
        back_ref[...] = jnp.zeros_like(back_ref)

    for jj in range(w_ref.shape[0]):
        j = step * w_ref.shape[0] + jj
        z = z_ref[:, jj * edge:(jj + 1) * edge]
        u = up_ref[:, pl.ds(pl.multiple_of(j * edge, edge), edge)].astype(jnp.float32)
        s = jax.nn.sigmoid(z)
        g = (u * s * (1.0 + z * (1.0 - s))).astype(jnp.bfloat16)
        g_ref[:, jj * edge:(jj + 1) * edge] = g
        spread = lax.dot_general(
            g,
            w_ref[jj].reshape(per_block * edge, edge),
            (((1,), (1,)), ((), ())),
            preferred_element_type=jnp.float32,
        )
        for k in range(per_block):
            c = cols_ref[j * per_block + k]
            at = pl.ds(pl.multiple_of(c * edge, edge), edge)
            back_ref[:, at] = back_ref[:, at] + spread[:, k * edge:(k + 1) * edge]

    @pl.when(step == pl.num_programs(0) - 1)
    def _():
        new_ref[...] = (up_ref[...].astype(jnp.float32) + back_ref[...]).astype(new_ref.dtype)


def layer_forward(cols, hidden, weight):
    rows, width = hidden.shape
    num_blocks, per_block, edge, _ = weight.shape
    grid = pltpu.PrefetchScalarGridSpec(
        num_scalar_prefetch=1,
        grid=(num_blocks // JB,),
        in_specs=[
            pl.BlockSpec((rows, width), lambda i, c: (0, 0)),
            pl.BlockSpec((JB, per_block, edge, edge), lambda i, c: (i, 0, 0, 0)),
        ],
        out_specs=[
            pl.BlockSpec((rows, JB * edge), lambda i, c: (0, i)),
            pl.BlockSpec((rows, JB * edge), lambda i, c: (0, i)),
        ],
    )
    flops = 2 * rows * num_blocks * per_block * edge * edge
    return pl.pallas_call(
        forward_kernel,
        grid_spec=grid,
        out_shape=[
            jax.ShapeDtypeStruct((rows, width), jnp.float32),
            jax.ShapeDtypeStruct((rows, width), hidden.dtype),
        ],
        compiler_params=pltpu.CompilerParams(dimension_semantics=("arbitrary",)),
        cost_estimate=pl.CostEstimate(
            flops=flops, transcendentals=rows * width, bytes_accessed=weight.size * 2 + rows * width * 8
        ),
    )(cols, hidden, weight)


def layer_backward(cols, upstream, preact, weight):
    rows, width = upstream.shape
    num_blocks, per_block, edge, _ = weight.shape
    grid = pltpu.PrefetchScalarGridSpec(
        num_scalar_prefetch=1,
        grid=(num_blocks // JB,),
        in_specs=[
            pl.BlockSpec((rows, width), lambda i, c: (0, 0)),
            pl.BlockSpec((rows, JB * edge), lambda i, c: (0, i)),
            pl.BlockSpec((JB, per_block, edge, edge), lambda i, c: (i, 0, 0, 0)),
        ],
        out_specs=[
            pl.BlockSpec((rows, JB * edge), lambda i, c: (0, i)),
            pl.BlockSpec((rows, width), lambda i, c: (0, 0)),
        ],
        scratch_shapes=[pltpu.VMEM((rows, width), jnp.float32)],
    )
    flops = 2 * rows * num_blocks * per_block * edge * edge
    return pl.pallas_call(
        backward_kernel,
        grid_spec=grid,
        out_shape=[
            jax.ShapeDtypeStruct((rows, width), jnp.bfloat16),
            jax.ShapeDtypeStruct((rows, width), upstream.dtype),
        ],
        compiler_params=pltpu.CompilerParams(dimension_semantics=("arbitrary",)),
        cost_estimate=pl.CostEstimate(
            flops=flops, transcendentals=rows * width, bytes_accessed=weight.size * 2 + rows * width * 10
        ),
    )(cols, upstream, preact, weight)


def grad_kernel(cols_ref, j_ref, h_ref, g_ref, out_ref):
    edge = out_ref.shape[-1]
    per_step = out_ref.shape[0]
    step = pl.program_id(0)
    for qq in range(per_step):
        q = step * per_step + qq
        c = cols_ref[q]
        x = h_ref[:, pl.ds(pl.multiple_of(c * edge, edge), edge)]
        j = j_ref[q]
        g = g_ref[:, pl.ds(pl.multiple_of(j * edge, edge), edge)]
        out_ref[qq] = lax.dot_general(
            x, g, (((0,), (0,)), ((), ())), preferred_element_type=jnp.float32
        )


def group_grads(cols, j_index, inputs_group, grads_group, pairs, per_step):
    rows, width = inputs_group.shape
    edge = 128
    grid = pltpu.PrefetchScalarGridSpec(
        num_scalar_prefetch=2,
        grid=(pairs // per_step,),
        in_specs=[
            pl.BlockSpec((rows, width), lambda i, c, j: (0, 0)),
            pl.BlockSpec(grads_group.shape, lambda i, c, j: (0, 0)),
        ],
        out_specs=pl.BlockSpec((per_step, edge, edge), lambda i, c, j: (i, 0, 0)),
    )
    return pl.pallas_call(
        grad_kernel,
        grid_spec=grid,
        out_shape=jax.ShapeDtypeStruct((pairs, edge, edge), jnp.float32),
        compiler_params=pltpu.CompilerParams(
            dimension_semantics=("arbitrary",), vmem_limit_bytes=48 * 1024 * 1024
        ),
        cost_estimate=pl.CostEstimate(
            flops=2 * rows * pairs * edge * edge,
            transcendentals=0,
            bytes_accessed=inputs_group.size * 2 + grads_group.size * 2 + pairs * edge * edge * 4,
        ),
    )(cols, j_index, inputs_group, grads_group)


def ring_reduce_scatter(chunks, axis, n):
    i = lax.axis_index(axis)
    half = chunks.shape[1] // 2
    east, west = chunks[:, :half], chunks[:, half:]
    cw = [(k, (k + 1) % n) for k in range(n)]
    ccw = [(k, (k - 1) % n) for k in range(n)]
    got_e = got_w = None
    for s in range(n - 1):
        send_e = lax.dynamic_index_in_dim(east, (i - s - 1) % n, 0, False)
        send_w = lax.dynamic_index_in_dim(west, (i + s + 1) % n, 0, False)
        if got_e is not None:
            send_e = got_e + send_e
            send_w = got_w + send_w
        got_e = lax.ppermute(send_e, axis, cw)
        got_w = lax.ppermute(send_w, axis, ccw)
    own_e = lax.dynamic_index_in_dim(east, i, 0, False)
    own_w = lax.dynamic_index_in_dim(west, i, 0, False)
    return jnp.concatenate([got_e + own_e, got_w + own_w], 0)


def body(inputs, cotangent, blocks, block_cols):
    segments = lax.axis_size("segment")
    segment_index = lax.axis_index("segment")
    weight = blocks[0]
    num_blocks, per_block, edge_size = (weight.shape[0], weight.shape[1], weight.shape[2])
    all_rows, layer_width = inputs.shape
    flat_cols = block_cols[0].reshape(-1)

    sides = DP_SIZES[1]
    middle = segments // 2

    def hop(block, src, dst):
        flip = (src < middle) != (dst < middle)
        route = [(src * sides + x, dst * sides + (sides - 1 - x if flip else x)) for x in range(sides)]
        return lax.ppermute(block, ("segment", "xlo"), route)

    zeros_x = jnp.zeros((all_rows, layer_width), jnp.bfloat16)
    zeros_z = jnp.zeros((all_rows, layer_width), jnp.float32)
    stash_x = inputs
    stash_z = zeros_z
    current = inputs
    for step_now in range(segments):
        active = segment_index == step_now
        held = current
        stash_z, result = lax.cond(
            active,
            lambda: layer_forward(flat_cols, held, weight),
            lambda: (stash_z, zeros_x),
        )
        if step_now > 0:
            stash_x = jnp.where(active, current, stash_x)
        if step_now + 1 < segments:
            current = hop(result, step_now, step_now + 1)
    stash_g = zeros_x
    last = segments - 1
    upstream = lax.ppermute(
        cotangent, ("segment", "xlo"), [(last * sides + x, last * sides + sides - 1 - x) for x in range(sides)]
    )
    for step_now in range(segments):
        owner = segments - 1 - step_now
        active = segment_index == owner
        held = upstream
        stash_g, passed = lax.cond(
            active,
            lambda: layer_backward(flat_cols, held, stash_z, weight),
            lambda: (stash_g, zeros_x),
        )
        if step_now + 1 < segments:
            upstream = hop(passed, owner, owner - 1)
    all_inputs = stash_x
    all_grads = stash_g
    ny, nx, nz = DP_SIZES
    members = ny
    group_pairs = num_blocks * per_block // members
    group_j = num_blocks // members
    member = lax.axis_index("y")
    grads_here = all_grads.reshape(all_rows, members, group_j * edge_size)
    pieces = [lax.dynamic_index_in_dim(grads_here, member, 1, False)]
    for offset in range(1, members):
        route = [(i, (i + offset) % members) for i in range(members)]
        outgoing = lax.dynamic_index_in_dim(grads_here, (member + offset) % members, 1, False)
        pieces.append(lax.ppermute(outgoing, "y", route))
    by_offset = jnp.stack(pieces)
    sender_offset = (member - jnp.arange(members, dtype=jnp.int32)) % members
    grads_group = jnp.take(by_offset, sender_offset, axis=0).reshape(
        members * all_rows, group_j * edge_size
    )
    inputs_group = lax.all_gather(all_inputs, "y", axis=0, tiled=True)
    cols_here = lax.dynamic_slice_in_dim(flat_cols, member * group_pairs, group_pairs)
    order = np.arange(group_pairs).reshape(nx, nz, -1).transpose(1, 0, 2).reshape(-1)
    j_index = jnp.asarray(order // per_block, jnp.int32)
    partial = group_grads(cols_here[order], j_index, inputs_group, grads_group, group_pairs, 16)
    reduced = ring_reduce_scatter(partial.reshape(nz, -1, edge_size), "z", nz)
    halves = reduced.reshape(nx, -1, edge_size)
    side = lax.axis_index("xlo")
    got = lax.ppermute(lax.dynamic_index_in_dim(halves, 1 - side, 0, False), "xlo", [(0, 1), (1, 0)])
    own_share = lax.dynamic_index_in_dim(halves, side, 0, False) + got
    summed = own_share.astype(jnp.bfloat16)
    return summed[None]


def solution(mesh):
    fine = Mesh(mesh.devices.reshape(mesh.shape["segment"], *DP_SIZES), ("segment",) + DP_AXES)
    return jax.shard_map(
        body,
        mesh=fine,
        in_specs=(
            P(DP_AXES, None),
            P(DP_AXES, None),
            P("segment", None, None, None, None),
            P("segment", None, None),
        ),
        out_specs=P("segment", DP_AXES, None),
        check_vma=False,
    )
```

```python
import functools

import jax
import jax.numpy as jnp
import numpy as np
from jax import lax
from jax.experimental import pallas as pl
from jax.experimental.pallas import tpu as pltpu
from jax.sharding import Mesh, PartitionSpec as P

DP_AXES = ("y", "xlo", "z")
DP_SIZES = (4, 2, 8)
JB = 16
PER_BLOCK = 8


def from_behind(block, axis, distance):
    devices = range(lax.axis_size(axis))
    route = [(i - distance, i) for i in devices if i - distance in devices]
    return lax.ppermute(block, axis, route)


def forward_kernel(cols_ref, h_ref, w_ref, z_ref, out_ref):
    edge = w_ref.shape[-1]
    per_block = w_ref.shape[1]
    step = pl.program_id(0)
    for jj in range(w_ref.shape[0]):
        j = step * w_ref.shape[0] + jj
        picked = jnp.concatenate(
            [
                h_ref[:, pl.ds(pl.multiple_of(cols_ref[j * per_block + k] * edge, edge), edge)]
                for k in range(per_block)
            ],
            axis=1,
        )
        acc = jnp.dot(
            picked, w_ref[jj].reshape(per_block * edge, edge), preferred_element_type=jnp.float32
        )
        z_ref[:, jj * edge:(jj + 1) * edge] = acc
        own = h_ref[:, pl.ds(pl.multiple_of(j * edge, edge), edge)].astype(jnp.float32)
        out_ref[:, jj * edge:(jj + 1) * edge] = (own + acc * jax.nn.sigmoid(acc)).astype(out_ref.dtype)


def backward_kernel(cols_ref, up_ref, z_ref, w_ref, g_ref, new_ref, back_ref):
    edge = w_ref.shape[-1]
    per_block = w_ref.shape[1]
    step = pl.program_id(0)

    @pl.when(step == 0)
    def _():
        back_ref[...] = jnp.zeros_like(back_ref)

    for jj in range(w_ref.shape[0]):
        j = step * w_ref.shape[0] + jj
        z = z_ref[:, jj * edge:(jj + 1) * edge]
        u = up_ref[:, pl.ds(pl.multiple_of(j * edge, edge), edge)].astype(jnp.float32)
        s = jax.nn.sigmoid(z)
        g = (u * s * (1.0 + z * (1.0 - s))).astype(jnp.bfloat16)
        g_ref[:, jj * edge:(jj + 1) * edge] = g
        spread = lax.dot_general(
            g,
            w_ref[jj].reshape(per_block * edge, edge),
            (((1,), (1,)), ((), ())),
            preferred_element_type=jnp.float32,
        )
        for k in range(per_block):
            c = cols_ref[j * per_block + k]
            at = pl.ds(pl.multiple_of(c * edge, edge), edge)
            back_ref[:, at] = back_ref[:, at] + spread[:, k * edge:(k + 1) * edge]

    @pl.when(step == pl.num_programs(0) - 1)
    def _():
        new_ref[...] = (up_ref[...].astype(jnp.float32) + back_ref[...]).astype(new_ref.dtype)


def layer_forward(cols, hidden, weight):
    rows, width = hidden.shape
    num_blocks, per_block, edge, _ = weight.shape
    grid = pltpu.PrefetchScalarGridSpec(
        num_scalar_prefetch=1,
        grid=(num_blocks // JB,),
        in_specs=[
            pl.BlockSpec((rows, width), lambda i, c: (0, 0)),
            pl.BlockSpec((JB, per_block, edge, edge), lambda i, c: (i, 0, 0, 0)),
        ],
        out_specs=[
            pl.BlockSpec((rows, JB * edge), lambda i, c: (0, i)),
            pl.BlockSpec((rows, JB * edge), lambda i, c: (0, i)),
        ],
    )
    flops = 2 * rows * num_blocks * per_block * edge * edge
    return pl.pallas_call(
        forward_kernel,
        grid_spec=grid,
        out_shape=[
            jax.ShapeDtypeStruct((rows, width), jnp.float32),
            jax.ShapeDtypeStruct((rows, width), hidden.dtype),
        ],
        compiler_params=pltpu.CompilerParams(dimension_semantics=("arbitrary",)),
        cost_estimate=pl.CostEstimate(
            flops=flops, transcendentals=rows * width, bytes_accessed=weight.size * 2 + rows * width * 8
        ),
    )(cols, hidden, weight)


def layer_backward(cols, upstream, preact, weight):
    rows, width = upstream.shape
    num_blocks, per_block, edge, _ = weight.shape
    grid = pltpu.PrefetchScalarGridSpec(
        num_scalar_prefetch=1,
        grid=(num_blocks // JB,),
        in_specs=[
            pl.BlockSpec((rows, width), lambda i, c: (0, 0)),
            pl.BlockSpec((rows, JB * edge), lambda i, c: (0, i)),
            pl.BlockSpec((JB, per_block, edge, edge), lambda i, c: (i, 0, 0, 0)),
        ],
        out_specs=[
            pl.BlockSpec((rows, JB * edge), lambda i, c: (0, i)),
            pl.BlockSpec((rows, width), lambda i, c: (0, 0)),
        ],
        scratch_shapes=[pltpu.VMEM((rows, width), jnp.float32)],
    )
    flops = 2 * rows * num_blocks * per_block * edge * edge
    return pl.pallas_call(
        backward_kernel,
        grid_spec=grid,
        out_shape=[
            jax.ShapeDtypeStruct((rows, width), jnp.bfloat16),
            jax.ShapeDtypeStruct((rows, width), upstream.dtype),
        ],
        compiler_params=pltpu.CompilerParams(dimension_semantics=("arbitrary",)),
        cost_estimate=pl.CostEstimate(
            flops=flops, transcendentals=rows * width, bytes_accessed=weight.size * 2 + rows * width * 10
        ),
    )(cols, upstream, preact, weight)


def grad_kernel(cols_ref, j_ref, h_ref, g_ref, out_ref):
    edge = out_ref.shape[-1]
    per_step = out_ref.shape[0]
    step = pl.program_id(0)
    for qq in range(per_step):
        q = step * per_step + qq
        c = cols_ref[q]
        x = h_ref[:, pl.ds(pl.multiple_of(c * edge, edge), edge)]
        j = j_ref[q]
        g = g_ref[:, pl.ds(pl.multiple_of(j * edge, edge), edge)]
        out_ref[qq] = lax.dot_general(
            x, g, (((0,), (0,)), ((), ())), preferred_element_type=jnp.float32
        )


def group_grads(cols, j_index, inputs_group, grads_group, pairs, per_step):
    rows, width = inputs_group.shape
    edge = 128
    grid = pltpu.PrefetchScalarGridSpec(
        num_scalar_prefetch=2,
        grid=(pairs // per_step,),
        in_specs=[
            pl.BlockSpec((rows, width), lambda i, c, j: (0, 0)),
            pl.BlockSpec(grads_group.shape, lambda i, c, j: (0, 0)),
        ],
        out_specs=pl.BlockSpec((per_step, edge, edge), lambda i, c, j: (i, 0, 0)),
    )
    return pl.pallas_call(
        grad_kernel,
        grid_spec=grid,
        out_shape=jax.ShapeDtypeStruct((pairs, edge, edge), jnp.float32),
        compiler_params=pltpu.CompilerParams(
            dimension_semantics=("arbitrary",), vmem_limit_bytes=48 * 1024 * 1024
        ),
        cost_estimate=pl.CostEstimate(
            flops=2 * rows * pairs * edge * edge,
            transcendentals=0,
            bytes_accessed=inputs_group.size * 2 + grads_group.size * 2 + pairs * edge * edge * 4,
        ),
    )(cols, j_index, inputs_group, grads_group)


def ring_reduce_scatter(chunks, axis, n):
    i = lax.axis_index(axis)
    half = chunks.shape[1] // 2
    east, west = chunks[:, :half], chunks[:, half:]
    cw = [(k, (k + 1) % n) for k in range(n)]
    ccw = [(k, (k - 1) % n) for k in range(n)]
    got_e = got_w = None
    for s in range(n - 1):
        send_e = lax.dynamic_index_in_dim(east, (i - s - 1) % n, 0, False)
        send_w = lax.dynamic_index_in_dim(west, (i + s + 1) % n, 0, False)
        if got_e is not None:
            send_e = got_e + send_e
            send_w = got_w + send_w
        got_e = lax.ppermute(send_e, axis, cw)
        got_w = lax.ppermute(send_w, axis, ccw)
    own_e = lax.dynamic_index_in_dim(east, i, 0, False)
    own_w = lax.dynamic_index_in_dim(west, i, 0, False)
    return jnp.concatenate([got_e + own_e, got_w + own_w], 0)


def body(inputs, cotangent, blocks, block_cols):
    segments = lax.axis_size("segment")
    segment_index = lax.axis_index("segment")
    weight = blocks[0]
    num_blocks, per_block, edge_size = (weight.shape[0], weight.shape[1], weight.shape[2])
    all_rows, layer_width = inputs.shape
    flat_cols = block_cols[0].reshape(-1)

    def hop(block, src, dst):
        return lax.ppermute(block, "segment", [(src, dst)])

    zeros_x = jnp.zeros((all_rows, layer_width), jnp.bfloat16)
    zeros_z = jnp.zeros((all_rows, layer_width), jnp.float32)
    stash_x = inputs
    stash_z = zeros_z
    current = inputs
    for step_now in range(segments):
        active = segment_index == step_now
        held = current
        stash_z, result = lax.cond(
            active,
            lambda: layer_forward(flat_cols, held, weight),
            lambda: (stash_z, zeros_x),
        )
        if step_now > 0:
            stash_x = jnp.where(active, current, stash_x)
        if step_now + 1 < segments:
            current = hop(result, step_now, step_now + 1)
    stash_g = zeros_x
    upstream = cotangent
    for step_now in range(segments):
        owner = segments - 1 - step_now
        active = segment_index == owner
        held = upstream
        stash_g, passed = lax.cond(
            active,
            lambda: layer_backward(flat_cols, held, stash_z, weight),
            lambda: (stash_g, zeros_x),
        )
        if step_now + 1 < segments:
            upstream = hop(passed, owner, owner - 1)
    all_inputs = stash_x
    all_grads = stash_g
    ny, nx, nz = DP_SIZES
    members = ny
    group_pairs = num_blocks * per_block // members
    group_j = num_blocks // members
    member = lax.axis_index("y")
    grads_here = all_grads.reshape(all_rows, members, group_j * edge_size)
    pieces = [lax.dynamic_index_in_dim(grads_here, member, 1, False)]
    for offset in range(1, members):
        route = [(i, (i + offset) % members) for i in range(members)]
        outgoing = lax.dynamic_index_in_dim(grads_here, (member + offset) % members, 1, False)
        pieces.append(lax.ppermute(outgoing, "y", route))
    by_offset = jnp.stack(pieces)
    sender_offset = (member - jnp.arange(members, dtype=jnp.int32)) % members
    grads_group = jnp.take(by_offset, sender_offset, axis=0).reshape(
        members * all_rows, group_j * edge_size
    )
    inputs_group = lax.all_gather(all_inputs, "y", axis=0, tiled=True)
    cols_here = lax.dynamic_slice_in_dim(flat_cols, member * group_pairs, group_pairs)
    order = np.arange(group_pairs).reshape(nx, nz, -1).transpose(1, 0, 2).reshape(-1)
    j_index = jnp.asarray(order // per_block, jnp.int32)
    partial = group_grads(cols_here[order], j_index, inputs_group, grads_group, group_pairs, 16)
    reduced = ring_reduce_scatter(partial.reshape(nz, -1, edge_size), "z", nz)
    halves = reduced.reshape(nx, -1, edge_size)
    side = lax.axis_index("xlo")
    got = lax.ppermute(lax.dynamic_index_in_dim(halves, 1 - side, 0, False), "xlo", [(0, 1), (1, 0)])
    own_share = lax.dynamic_index_in_dim(halves, side, 0, False) + got
    summed = own_share.astype(jnp.bfloat16)
    return summed[None]


def solution(mesh):
    fine = Mesh(mesh.devices.reshape(mesh.shape["segment"], *DP_SIZES), ("segment",) + DP_AXES)
    return jax.shard_map(
        body,
        mesh=fine,
        in_specs=(
            P(DP_AXES, None),
            P(DP_AXES, None),
            P("segment", None, None, None, None),
            P("segment", None, None),
        ),
        out_specs=P("segment", DP_AXES, None),
        check_vma=False,
    )
```

```python
import functools

import jax
import jax.numpy as jnp
import numpy as np
from jax import lax
from jax.experimental import pallas as pl
from jax.experimental.pallas import tpu as pltpu
from jax.sharding import Mesh, PartitionSpec as P

DP_AXES = ("y", "xlo", "z")
DP_SIZES = (4, 2, 8)
JB = 8
PER_BLOCK = 8


def from_behind(block, axis, distance):
    devices = range(lax.axis_size(axis))
    route = [(i - distance, i) for i in devices if i - distance in devices]
    return lax.ppermute(block, axis, route)


def forward_kernel(cols_ref, h_ref, w_ref, z_ref, out_ref):
    edge = w_ref.shape[-1]
    per_block = w_ref.shape[1]
    step = pl.program_id(0)
    for jj in range(w_ref.shape[0]):
        j = step * w_ref.shape[0] + jj
        picked = jnp.concatenate(
            [
                h_ref[:, pl.ds(pl.multiple_of(cols_ref[j * per_block + k] * edge, edge), edge)]
                for k in range(per_block)
            ],
            axis=1,
        )
        acc = jnp.dot(
            picked, w_ref[jj].reshape(per_block * edge, edge), preferred_element_type=jnp.float32
        )
        z_ref[:, jj * edge:(jj + 1) * edge] = acc
        own = h_ref[:, pl.ds(pl.multiple_of(j * edge, edge), edge)].astype(jnp.float32)
        out_ref[:, jj * edge:(jj + 1) * edge] = (own + acc * jax.nn.sigmoid(acc)).astype(out_ref.dtype)


def backward_kernel(cols_ref, up_ref, z_ref, w_ref, g_ref, new_ref, back_ref):
    edge = w_ref.shape[-1]
    per_block = w_ref.shape[1]
    step = pl.program_id(0)

    @pl.when(step == 0)
    def _():
        back_ref[...] = jnp.zeros_like(back_ref)

    for jj in range(w_ref.shape[0]):
        j = step * w_ref.shape[0] + jj
        z = z_ref[:, jj * edge:(jj + 1) * edge]
        u = up_ref[:, pl.ds(pl.multiple_of(j * edge, edge), edge)].astype(jnp.float32)
        s = jax.nn.sigmoid(z)
        g = (u * s * (1.0 + z * (1.0 - s))).astype(jnp.bfloat16)
        g_ref[:, jj * edge:(jj + 1) * edge] = g
        spread = lax.dot_general(
            g,
            w_ref[jj].reshape(per_block * edge, edge),
            (((1,), (1,)), ((), ())),
            preferred_element_type=jnp.float32,
        )
        for k in range(per_block):
            c = cols_ref[j * per_block + k]
            at = pl.ds(pl.multiple_of(c * edge, edge), edge)
            back_ref[:, at] = back_ref[:, at] + spread[:, k * edge:(k + 1) * edge]

    @pl.when(step == pl.num_programs(0) - 1)
    def _():
        new_ref[...] = (up_ref[...].astype(jnp.float32) + back_ref[...]).astype(new_ref.dtype)


def layer_forward(cols, hidden, weight):
    rows, width = hidden.shape
    num_blocks, per_block, edge, _ = weight.shape
    grid = pltpu.PrefetchScalarGridSpec(
        num_scalar_prefetch=1,
        grid=(num_blocks // JB,),
        in_specs=[
            pl.BlockSpec((rows, width), lambda i, c: (0, 0)),
            pl.BlockSpec((JB, per_block, edge, edge), lambda i, c: (i, 0, 0, 0)),
        ],
        out_specs=[
            pl.BlockSpec((rows, JB * edge), lambda i, c: (0, i)),
            pl.BlockSpec((rows, JB * edge), lambda i, c: (0, i)),
        ],
    )
    flops = 2 * rows * num_blocks * per_block * edge * edge
    return pl.pallas_call(
        forward_kernel,
        grid_spec=grid,
        out_shape=[
            jax.ShapeDtypeStruct((rows, width), jnp.float32),
            jax.ShapeDtypeStruct((rows, width), hidden.dtype),
        ],
        compiler_params=pltpu.CompilerParams(dimension_semantics=("arbitrary",)),
        cost_estimate=pl.CostEstimate(
            flops=flops, transcendentals=rows * width, bytes_accessed=weight.size * 2 + rows * width * 8
        ),
    )(cols, hidden, weight)


def layer_backward(cols, upstream, preact, weight):
    rows, width = upstream.shape
    num_blocks, per_block, edge, _ = weight.shape
    grid = pltpu.PrefetchScalarGridSpec(
        num_scalar_prefetch=1,
        grid=(num_blocks // JB,),
        in_specs=[
            pl.BlockSpec((rows, width), lambda i, c: (0, 0)),
            pl.BlockSpec((rows, JB * edge), lambda i, c: (0, i)),
            pl.BlockSpec((JB, per_block, edge, edge), lambda i, c: (i, 0, 0, 0)),
        ],
        out_specs=[
            pl.BlockSpec((rows, JB * edge), lambda i, c: (0, i)),
            pl.BlockSpec((rows, width), lambda i, c: (0, 0)),
        ],
        scratch_shapes=[pltpu.VMEM((rows, width), jnp.float32)],
    )
    flops = 2 * rows * num_blocks * per_block * edge * edge
    return pl.pallas_call(
        backward_kernel,
        grid_spec=grid,
        out_shape=[
            jax.ShapeDtypeStruct((rows, width), jnp.bfloat16),
            jax.ShapeDtypeStruct((rows, width), upstream.dtype),
        ],
        compiler_params=pltpu.CompilerParams(dimension_semantics=("arbitrary",)),
        cost_estimate=pl.CostEstimate(
            flops=flops, transcendentals=rows * width, bytes_accessed=weight.size * 2 + rows * width * 10
        ),
    )(cols, upstream, preact, weight)


def grad_kernel(cols_ref, j_ref, h_ref, g_ref, out_ref):
    edge = out_ref.shape[-1]
    per_step = out_ref.shape[0]
    step = pl.program_id(0)
    for qq in range(per_step):
        q = step * per_step + qq
        c = cols_ref[q]
        x = h_ref[:, pl.ds(pl.multiple_of(c * edge, edge), edge)]
        j = j_ref[q]
        g = g_ref[:, pl.ds(pl.multiple_of(j * edge, edge), edge)]
        out_ref[qq] = lax.dot_general(
            x, g, (((0,), (0,)), ((), ())), preferred_element_type=jnp.float32
        )


def group_grads(cols, j_index, inputs_group, grads_group, pairs, per_step):
    rows, width = inputs_group.shape
    edge = 128
    grid = pltpu.PrefetchScalarGridSpec(
        num_scalar_prefetch=2,
        grid=(pairs // per_step,),
        in_specs=[
            pl.BlockSpec((rows, width), lambda i, c, j: (0, 0)),
            pl.BlockSpec(grads_group.shape, lambda i, c, j: (0, 0)),
        ],
        out_specs=pl.BlockSpec((per_step, edge, edge), lambda i, c, j: (i, 0, 0)),
    )
    return pl.pallas_call(
        grad_kernel,
        grid_spec=grid,
        out_shape=jax.ShapeDtypeStruct((pairs, edge, edge), jnp.float32),
        compiler_params=pltpu.CompilerParams(
            dimension_semantics=("arbitrary",), vmem_limit_bytes=48 * 1024 * 1024
        ),
        cost_estimate=pl.CostEstimate(
            flops=2 * rows * pairs * edge * edge,
            transcendentals=0,
            bytes_accessed=inputs_group.size * 2 + grads_group.size * 2 + pairs * edge * edge * 4,
        ),
    )(cols, j_index, inputs_group, grads_group)


def ring_reduce_scatter(chunks, axis, n):
    i = lax.axis_index(axis)
    cw = [(k, (k + 1) % n) for k in range(n)]
    got = None
    for s in range(n - 1):
        send = lax.dynamic_index_in_dim(chunks, (i - s - 1) % n, 0, False)
        if got is not None:
            send = got + send
        got = lax.ppermute(send, axis, cw)
    return got + lax.dynamic_index_in_dim(chunks, i, 0, False)


def body(inputs, cotangent, blocks, block_cols):
    segments = lax.axis_size("segment")
    segment_index = lax.axis_index("segment")
    weight = blocks[0]
    num_blocks, per_block, edge_size = (weight.shape[0], weight.shape[1], weight.shape[2])
    all_rows, layer_width = inputs.shape
    flat_cols = block_cols[0].reshape(-1)

    def hop(block, src, dst):
        return lax.ppermute(block, "segment", [(src, dst)])

    zeros_x = jnp.zeros((all_rows, layer_width), jnp.bfloat16)
    zeros_z = jnp.zeros((all_rows, layer_width), jnp.float32)
    stash_x = inputs
    stash_z = zeros_z
    current = inputs
    for step_now in range(segments):
        active = segment_index == step_now
        held = current
        stash_z, result = lax.cond(
            active,
            lambda: layer_forward(flat_cols, held, weight),
            lambda: (stash_z, zeros_x),
        )
        if step_now > 0:
            stash_x = jnp.where(active, current, stash_x)
        if step_now + 1 < segments:
            current = hop(result, step_now, step_now + 1)
    stash_g = zeros_x
    upstream = cotangent
    for step_now in range(segments):
        owner = segments - 1 - step_now
        active = segment_index == owner
        held = upstream
        stash_g, passed = lax.cond(
            active,
            lambda: layer_backward(flat_cols, held, stash_z, weight),
            lambda: (stash_g, zeros_x),
        )
        if step_now + 1 < segments:
            upstream = hop(passed, owner, owner - 1)
    all_inputs = stash_x
    all_grads = stash_g
    ny, nx, nz = DP_SIZES
    members = ny
    group_pairs = num_blocks * per_block // members
    group_j = num_blocks // members
    member = lax.axis_index("y")
    grads_here = all_grads.reshape(all_rows, members, group_j * edge_size)
    pieces = [lax.dynamic_index_in_dim(grads_here, member, 1, False)]
    for offset in range(1, members):
        route = [(i, (i + offset) % members) for i in range(members)]
        outgoing = lax.dynamic_index_in_dim(grads_here, (member + offset) % members, 1, False)
        pieces.append(lax.ppermute(outgoing, "y", route))
    by_offset = jnp.stack(pieces)
    sender_offset = (member - jnp.arange(members, dtype=jnp.int32)) % members
    grads_group = jnp.take(by_offset, sender_offset, axis=0).reshape(
        members * all_rows, group_j * edge_size
    )
    inputs_group = lax.all_gather(all_inputs, "y", axis=0, tiled=True)
    cols_here = lax.dynamic_slice_in_dim(flat_cols, member * group_pairs, group_pairs)
    order = np.arange(group_pairs).reshape(nx, nz, -1).transpose(1, 0, 2).reshape(-1)
    j_index = jnp.asarray(order // per_block, jnp.int32)
    partial = group_grads(cols_here[order], j_index, inputs_group, grads_group, group_pairs, 16)
    reduced = ring_reduce_scatter(partial.reshape(nz, -1, edge_size), "z", nz)
    halves = reduced.reshape(nx, -1, edge_size)
    side = lax.axis_index("xlo")
    got = lax.ppermute(lax.dynamic_index_in_dim(halves, 1 - side, 0, False), "xlo", [(0, 1), (1, 0)])
    own_share = lax.dynamic_index_in_dim(halves, side, 0, False) + got
    summed = own_share.astype(jnp.bfloat16)
    return summed[None]


def solution(mesh):
    fine = Mesh(mesh.devices.reshape(mesh.shape["segment"], *DP_SIZES), ("segment",) + DP_AXES)
    return jax.shard_map(
        body,
        mesh=fine,
        in_specs=(
            P(DP_AXES, None),
            P(DP_AXES, None),
            P("segment", None, None, None, None),
            P("segment", None, None),
        ),
        out_specs=P("segment", DP_AXES, None),
        check_vma=False,
    )
```

```python
import functools

import jax
import jax.numpy as jnp
import numpy as np
from jax import lax
from jax.experimental import pallas as pl
from jax.experimental.pallas import tpu as pltpu
from jax.sharding import Mesh, PartitionSpec as P

DP_AXES = ("y", "xlo", "z")
DP_SIZES = (4, 2, 8)
JB = 8
PER_BLOCK = 8


def from_behind(block, axis, distance):
    devices = range(lax.axis_size(axis))
    route = [(i - distance, i) for i in devices if i - distance in devices]
    return lax.ppermute(block, axis, route)


def forward_kernel(cols_ref, h_ref, w_ref, z_ref, out_ref):
    edge = w_ref.shape[-1]
    per_block = w_ref.shape[1]
    step = pl.program_id(0)
    for jj in range(w_ref.shape[0]):
        j = step * w_ref.shape[0] + jj
        picked = jnp.concatenate(
            [
                h_ref[:, pl.ds(pl.multiple_of(cols_ref[j * per_block + k] * edge, edge), edge)]
                for k in range(per_block)
            ],
            axis=1,
        )
        acc = jnp.dot(
            picked, w_ref[jj].reshape(per_block * edge, edge), preferred_element_type=jnp.float32
        )
        z_ref[:, jj * edge:(jj + 1) * edge] = acc
        own = h_ref[:, pl.ds(pl.multiple_of(j * edge, edge), edge)].astype(jnp.float32)
        out_ref[:, jj * edge:(jj + 1) * edge] = (own + acc * jax.nn.sigmoid(acc)).astype(out_ref.dtype)


def backward_kernel(cols_ref, up_ref, z_ref, w_ref, g_ref, new_ref, back_ref):
    edge = w_ref.shape[-1]
    per_block = w_ref.shape[1]
    step = pl.program_id(0)

    @pl.when(step == 0)
    def _():
        back_ref[...] = jnp.zeros_like(back_ref)

    for jj in range(w_ref.shape[0]):
        j = step * w_ref.shape[0] + jj
        z = z_ref[:, jj * edge:(jj + 1) * edge]
        u = up_ref[:, pl.ds(pl.multiple_of(j * edge, edge), edge)].astype(jnp.float32)
        s = jax.nn.sigmoid(z)
        g = (u * s * (1.0 + z * (1.0 - s))).astype(jnp.bfloat16)
        g_ref[:, jj * edge:(jj + 1) * edge] = g
        spread = lax.dot_general(
            g,
            w_ref[jj].reshape(per_block * edge, edge),
            (((1,), (1,)), ((), ())),
            preferred_element_type=jnp.float32,
        )
        for k in range(per_block):
            c = cols_ref[j * per_block + k]
            at = pl.ds(pl.multiple_of(c * edge, edge), edge)
            back_ref[:, at] = back_ref[:, at] + spread[:, k * edge:(k + 1) * edge]

    @pl.when(step == pl.num_programs(0) - 1)
    def _():
        new_ref[...] = (up_ref[...].astype(jnp.float32) + back_ref[...]).astype(new_ref.dtype)


def layer_forward(cols, hidden, weight):
    rows, width = hidden.shape
    num_blocks, per_block, edge, _ = weight.shape
    grid = pltpu.PrefetchScalarGridSpec(
        num_scalar_prefetch=1,
        grid=(num_blocks // JB,),
        in_specs=[
            pl.BlockSpec((rows, width), lambda i, c: (0, 0)),
            pl.BlockSpec((JB, per_block, edge, edge), lambda i, c: (i, 0, 0, 0)),
        ],
        out_specs=[
            pl.BlockSpec((rows, JB * edge), lambda i, c: (0, i)),
            pl.BlockSpec((rows, JB * edge), lambda i, c: (0, i)),
        ],
    )
    flops = 2 * rows * num_blocks * per_block * edge * edge
    return pl.pallas_call(
        forward_kernel,
        grid_spec=grid,
        out_shape=[
            jax.ShapeDtypeStruct((rows, width), jnp.float32),
            jax.ShapeDtypeStruct((rows, width), hidden.dtype),
        ],
        compiler_params=pltpu.CompilerParams(dimension_semantics=("arbitrary",)),
        cost_estimate=pl.CostEstimate(
            flops=flops, transcendentals=rows * width, bytes_accessed=weight.size * 2 + rows * width * 8
        ),
    )(cols, hidden, weight)


def layer_backward(cols, upstream, preact, weight):
    rows, width = upstream.shape
    num_blocks, per_block, edge, _ = weight.shape
    grid = pltpu.PrefetchScalarGridSpec(
        num_scalar_prefetch=1,
        grid=(num_blocks // JB,),
        in_specs=[
            pl.BlockSpec((rows, width), lambda i, c: (0, 0)),
            pl.BlockSpec((rows, JB * edge), lambda i, c: (0, i)),
            pl.BlockSpec((JB, per_block, edge, edge), lambda i, c: (i, 0, 0, 0)),
        ],
        out_specs=[
            pl.BlockSpec((rows, JB * edge), lambda i, c: (0, i)),
            pl.BlockSpec((rows, width), lambda i, c: (0, 0)),
        ],
        scratch_shapes=[pltpu.VMEM((rows, width), jnp.float32)],
    )
    flops = 2 * rows * num_blocks * per_block * edge * edge
    return pl.pallas_call(
        backward_kernel,
        grid_spec=grid,
        out_shape=[
            jax.ShapeDtypeStruct((rows, width), jnp.bfloat16),
            jax.ShapeDtypeStruct((rows, width), upstream.dtype),
        ],
        compiler_params=pltpu.CompilerParams(dimension_semantics=("arbitrary",)),
        cost_estimate=pl.CostEstimate(
            flops=flops, transcendentals=rows * width, bytes_accessed=weight.size * 2 + rows * width * 10
        ),
    )(cols, upstream, preact, weight)


def grad_kernel(cols_ref, j_ref, h_ref, g_ref, out_ref):
    edge = out_ref.shape[-1]
    per_step = out_ref.shape[0]
    step = pl.program_id(0)
    for qq in range(per_step):
        q = step * per_step + qq
        c = cols_ref[q]
        x = h_ref[:, pl.ds(pl.multiple_of(c * edge, edge), edge)]
        j = j_ref[q]
        g = g_ref[:, pl.ds(pl.multiple_of(j * edge, edge), edge)]
        out_ref[qq] = lax.dot_general(
            x, g, (((0,), (0,)), ((), ())), preferred_element_type=jnp.float32
        )


def group_grads(cols, j_index, inputs_group, grads_group, pairs, per_step):
    rows, width = inputs_group.shape
    edge = 128
    grid = pltpu.PrefetchScalarGridSpec(
        num_scalar_prefetch=2,
        grid=(pairs // per_step,),
        in_specs=[
            pl.BlockSpec((rows, width), lambda i, c, j: (0, 0)),
            pl.BlockSpec(grads_group.shape, lambda i, c, j: (0, 0)),
        ],
        out_specs=pl.BlockSpec((per_step, edge, edge), lambda i, c, j: (i, 0, 0)),
    )
    return pl.pallas_call(
        grad_kernel,
        grid_spec=grid,
        out_shape=jax.ShapeDtypeStruct((pairs, edge, edge), jnp.float32),
        compiler_params=pltpu.CompilerParams(
            dimension_semantics=("arbitrary",), vmem_limit_bytes=48 * 1024 * 1024
        ),
        cost_estimate=pl.CostEstimate(
            flops=2 * rows * pairs * edge * edge,
            transcendentals=0,
            bytes_accessed=inputs_group.size * 2 + grads_group.size * 2 + pairs * edge * edge * 4,
        ),
    )(cols, j_index, inputs_group, grads_group)


def ring_reduce_scatter(chunks, axis, n):
    i = lax.axis_index(axis)
    half = chunks.shape[1] // 2
    east, west = chunks[:, :half], chunks[:, half:]
    cw = [(k, (k + 1) % n) for k in range(n)]
    ccw = [(k, (k - 1) % n) for k in range(n)]
    got_e = got_w = None
    for s in range(n - 1):
        send_e = lax.dynamic_index_in_dim(east, (i - s - 1) % n, 0, False)
        send_w = lax.dynamic_index_in_dim(west, (i + s + 1) % n, 0, False)
        if got_e is not None:
            send_e = got_e + send_e
            send_w = got_w + send_w
        got_e = lax.ppermute(send_e, axis, cw)
        got_w = lax.ppermute(send_w, axis, ccw)
    own_e = lax.dynamic_index_in_dim(east, i, 0, False)
    own_w = lax.dynamic_index_in_dim(west, i, 0, False)
    return jnp.concatenate([got_e + own_e, got_w + own_w], 0)


def body(inputs, cotangent, blocks, block_cols):
    segments = lax.axis_size("segment")
    segment_index = lax.axis_index("segment")
    weight = blocks[0]
    num_blocks, per_block, edge_size = (weight.shape[0], weight.shape[1], weight.shape[2])
    all_rows, layer_width = inputs.shape
    flat_cols = block_cols[0].reshape(-1)

    def hop(block, src, dst):
        return lax.ppermute(block, "segment", [(src, dst)])

    zeros_x = jnp.zeros((all_rows, layer_width), jnp.bfloat16)
    zeros_z = jnp.zeros((all_rows, layer_width), jnp.float32)
    stash_x = inputs
    stash_z = zeros_z
    current = inputs
    for step_now in range(segments):
        active = segment_index == step_now
        held = current
        stash_z, result = lax.cond(
            active,
            lambda: layer_forward(flat_cols, held, weight),
            lambda: (stash_z, zeros_x),
        )
        if step_now > 0:
            stash_x = jnp.where(active, current, stash_x)
        if step_now + 1 < segments:
            current = hop(result, step_now, step_now + 1)
    stash_g = zeros_x
    upstream = cotangent
    for step_now in range(segments):
        owner = segments - 1 - step_now
        active = segment_index == owner
        held = upstream
        stash_g, passed = lax.cond(
            active,
            lambda: layer_backward(flat_cols, held, stash_z, weight),
            lambda: (stash_g, zeros_x),
        )
        if step_now + 1 < segments:
            upstream = hop(passed, owner, owner - 1)
    all_inputs = stash_x
    all_grads = stash_g
    ny, nx, nz = DP_SIZES
    members = ny
    group_pairs = num_blocks * per_block // members
    group_j = num_blocks // members
    member = lax.axis_index("y")
    grads_here = all_grads.reshape(all_rows, members, group_j * edge_size)
    pieces = [lax.dynamic_index_in_dim(grads_here, member, 1, False)]
    for offset in range(1, members):
        route = [(i, (i + offset) % members) for i in range(members)]
        outgoing = lax.dynamic_index_in_dim(grads_here, (member + offset) % members, 1, False)
        pieces.append(lax.ppermute(outgoing, "y", route))
    by_offset = jnp.stack(pieces)
    sender_offset = (member - jnp.arange(members, dtype=jnp.int32)) % members
    grads_group = jnp.take(by_offset, sender_offset, axis=0).reshape(
        members * all_rows, group_j * edge_size
    )
    inputs_group = lax.all_gather(all_inputs, "y", axis=0, tiled=True)
    cols_here = lax.dynamic_slice_in_dim(flat_cols, member * group_pairs, group_pairs)
    order = np.arange(group_pairs).reshape(nx, nz, -1).transpose(1, 0, 2).reshape(-1)
    j_index = jnp.asarray(order // per_block, jnp.int32)
    partial = group_grads(cols_here[order], j_index, inputs_group, grads_group, group_pairs, 32)
    reduced = ring_reduce_scatter(partial.reshape(nz, -1, edge_size), "z", nz)
    halves = reduced.reshape(nx, -1, edge_size)
    side = lax.axis_index("xlo")
    got = lax.ppermute(lax.dynamic_index_in_dim(halves, 1 - side, 0, False), "xlo", [(0, 1), (1, 0)])
    own_share = lax.dynamic_index_in_dim(halves, side, 0, False) + got
    summed = own_share.astype(jnp.bfloat16)
    return summed[None]


def solution(mesh):
    fine = Mesh(mesh.devices.reshape(mesh.shape["segment"], *DP_SIZES), ("segment",) + DP_AXES)
    return jax.shard_map(
        body,
        mesh=fine,
        in_specs=(
            P(DP_AXES, None),
            P(DP_AXES, None),
            P("segment", None, None, None, None),
            P("segment", None, None),
        ),
        out_specs=P("segment", DP_AXES, None),
        check_vma=False,
    )
```

```python
import functools

import jax
import jax.numpy as jnp
import numpy as np
from jax import lax
from jax.experimental import pallas as pl
from jax.experimental.pallas import tpu as pltpu
from jax.sharding import Mesh, PartitionSpec as P

DP_AXES = ("y", "xlo", "z")
DP_SIZES = (4, 2, 8)
JB = 8
PER_BLOCK = 8


def from_behind(block, axis, distance):
    devices = range(lax.axis_size(axis))
    route = [(i - distance, i) for i in devices if i - distance in devices]
    return lax.ppermute(block, axis, route)


def forward_kernel(cols_ref, h_ref, w_ref, z_ref, out_ref):
    edge = w_ref.shape[-1]
    per_block = w_ref.shape[1]
    step = pl.program_id(0)
    for jj in range(w_ref.shape[0]):
        j = step * w_ref.shape[0] + jj
        picked = jnp.concatenate(
            [
                h_ref[:, pl.ds(pl.multiple_of(cols_ref[j * per_block + k] * edge, edge), edge)]
                for k in range(per_block)
            ],
            axis=1,
        )
        acc = jnp.dot(
            picked, w_ref[jj].reshape(per_block * edge, edge), preferred_element_type=jnp.float32
        )
        z_ref[:, jj * edge:(jj + 1) * edge] = acc
        own = h_ref[:, pl.ds(pl.multiple_of(j * edge, edge), edge)].astype(jnp.float32)
        out_ref[:, jj * edge:(jj + 1) * edge] = (own + acc * jax.nn.sigmoid(acc)).astype(out_ref.dtype)


def backward_kernel(cols_ref, up_ref, z_ref, w_ref, g_ref, new_ref, back_ref):
    edge = w_ref.shape[-1]
    per_block = w_ref.shape[1]
    step = pl.program_id(0)

    @pl.when(step == 0)
    def _():
        back_ref[...] = jnp.zeros_like(back_ref)

    for jj in range(w_ref.shape[0]):
        j = step * w_ref.shape[0] + jj
        z = z_ref[:, jj * edge:(jj + 1) * edge]
        u = up_ref[:, pl.ds(pl.multiple_of(j * edge, edge), edge)].astype(jnp.float32)
        s = jax.nn.sigmoid(z)
        g = (u * s * (1.0 + z * (1.0 - s))).astype(jnp.bfloat16)
        g_ref[:, jj * edge:(jj + 1) * edge] = g
        spread = lax.dot_general(
            g,
            w_ref[jj].reshape(per_block * edge, edge),
            (((1,), (1,)), ((), ())),
            preferred_element_type=jnp.float32,
        )
        for k in range(per_block):
            c = cols_ref[j * per_block + k]
            at = pl.ds(pl.multiple_of(c * edge, edge), edge)
            back_ref[:, at] = back_ref[:, at] + spread[:, k * edge:(k + 1) * edge]

    @pl.when(step == pl.num_programs(0) - 1)
    def _():
        new_ref[...] = (up_ref[...].astype(jnp.float32) + back_ref[...]).astype(new_ref.dtype)


def layer_forward(cols, hidden, weight):
    rows, width = hidden.shape
    num_blocks, per_block, edge, _ = weight.shape
    grid = pltpu.PrefetchScalarGridSpec(
        num_scalar_prefetch=1,
        grid=(num_blocks // JB,),
        in_specs=[
            pl.BlockSpec((rows, width), lambda i, c: (0, 0)),
            pl.BlockSpec((JB, per_block, edge, edge), lambda i, c: (i, 0, 0, 0)),
        ],
        out_specs=[
            pl.BlockSpec((rows, JB * edge), lambda i, c: (0, i)),
            pl.BlockSpec((rows, JB * edge), lambda i, c: (0, i)),
        ],
    )
    flops = 2 * rows * num_blocks * per_block * edge * edge
    return pl.pallas_call(
        forward_kernel,
        grid_spec=grid,
        out_shape=[
            jax.ShapeDtypeStruct((rows, width), jnp.float32),
            jax.ShapeDtypeStruct((rows, width), hidden.dtype),
        ],
        compiler_params=pltpu.CompilerParams(dimension_semantics=("arbitrary",)),
        cost_estimate=pl.CostEstimate(
            flops=flops, transcendentals=rows * width, bytes_accessed=weight.size * 2 + rows * width * 8
        ),
    )(cols, hidden, weight)


def layer_backward(cols, upstream, preact, weight):
    rows, width = upstream.shape
    num_blocks, per_block, edge, _ = weight.shape
    grid = pltpu.PrefetchScalarGridSpec(
        num_scalar_prefetch=1,
        grid=(num_blocks // JB,),
        in_specs=[
            pl.BlockSpec((rows, width), lambda i, c: (0, 0)),
            pl.BlockSpec((rows, JB * edge), lambda i, c: (0, i)),
            pl.BlockSpec((JB, per_block, edge, edge), lambda i, c: (i, 0, 0, 0)),
        ],
        out_specs=[
            pl.BlockSpec((rows, JB * edge), lambda i, c: (0, i)),
            pl.BlockSpec((rows, width), lambda i, c: (0, 0)),
        ],
        scratch_shapes=[pltpu.VMEM((rows, width), jnp.float32)],
    )
    flops = 2 * rows * num_blocks * per_block * edge * edge
    return pl.pallas_call(
        backward_kernel,
        grid_spec=grid,
        out_shape=[
            jax.ShapeDtypeStruct((rows, width), jnp.bfloat16),
            jax.ShapeDtypeStruct((rows, width), upstream.dtype),
        ],
        compiler_params=pltpu.CompilerParams(dimension_semantics=("arbitrary",)),
        cost_estimate=pl.CostEstimate(
            flops=flops, transcendentals=rows * width, bytes_accessed=weight.size * 2 + rows * width * 10
        ),
    )(cols, upstream, preact, weight)


def grad_kernel(cols_ref, j_ref, h_ref, g_ref, out_ref):
    edge = out_ref.shape[-1]
    per_step = out_ref.shape[0]
    step = pl.program_id(0)
    for qq in range(per_step):
        q = step * per_step + qq
        c = cols_ref[q]
        x = h_ref[:, pl.ds(pl.multiple_of(c * edge, edge), edge)]
        j = j_ref[q]
        g = g_ref[:, pl.ds(pl.multiple_of(j * edge, edge), edge)]
        out_ref[qq] = lax.dot_general(
            x, g, (((0,), (0,)), ((), ())), preferred_element_type=jnp.float32
        )


def group_grads(cols, j_index, inputs_group, grads_group, pairs, per_step):
    rows, width = inputs_group.shape
    edge = 128
    grid = pltpu.PrefetchScalarGridSpec(
        num_scalar_prefetch=2,
        grid=(pairs // per_step,),
        in_specs=[
            pl.BlockSpec((rows, width), lambda i, c, j: (0, 0)),
            pl.BlockSpec(grads_group.shape, lambda i, c, j: (0, 0)),
        ],
        out_specs=pl.BlockSpec((per_step, edge, edge), lambda i, c, j: (i, 0, 0)),
    )
    return pl.pallas_call(
        grad_kernel,
        grid_spec=grid,
        out_shape=jax.ShapeDtypeStruct((pairs, edge, edge), jnp.float32),
        compiler_params=pltpu.CompilerParams(
            dimension_semantics=("arbitrary",), vmem_limit_bytes=48 * 1024 * 1024
        ),
        cost_estimate=pl.CostEstimate(
            flops=2 * rows * pairs * edge * edge,
            transcendentals=0,
            bytes_accessed=inputs_group.size * 2 + grads_group.size * 2 + pairs * edge * edge * 4,
        ),
    )(cols, j_index, inputs_group, grads_group)


def ring_reduce_scatter(chunks, axis, n):
    i = lax.axis_index(axis)
    half = chunks.shape[1] // 2
    east, west = chunks[:, :half], chunks[:, half:]
    cw = [(k, (k + 1) % n) for k in range(n)]
    ccw = [(k, (k - 1) % n) for k in range(n)]
    got_e = got_w = None
    for s in range(n - 1):
        send_e = lax.dynamic_index_in_dim(east, (i - s - 1) % n, 0, False)
        send_w = lax.dynamic_index_in_dim(west, (i + s + 1) % n, 0, False)
        if got_e is not None:
            send_e = got_e + send_e
            send_w = got_w + send_w
        got_e = lax.ppermute(send_e, axis, cw)
        got_w = lax.ppermute(send_w, axis, ccw)
    own_e = lax.dynamic_index_in_dim(east, i, 0, False)
    own_w = lax.dynamic_index_in_dim(west, i, 0, False)
    return jnp.concatenate([got_e + own_e, got_w + own_w], 0)


def body(inputs, cotangent, blocks, block_cols):
    segments = lax.axis_size("segment")
    segment_index = lax.axis_index("segment")
    weight = blocks[0]
    num_blocks, per_block, edge_size = (weight.shape[0], weight.shape[1], weight.shape[2])
    all_rows, layer_width = inputs.shape
    flat_cols = block_cols[0].reshape(-1)

    def hop(block, src, dst):
        return lax.ppermute(block, "segment", [(src, dst)])

    zeros_x = jnp.zeros((all_rows, layer_width), jnp.bfloat16)
    zeros_z = jnp.zeros((all_rows, layer_width), jnp.float32)
    stash_x = inputs
    stash_z = zeros_z
    current = inputs
    for step_now in range(segments):
        active = segment_index == step_now
        held = current
        stash_z, result = lax.cond(
            active,
            lambda: layer_forward(flat_cols, held, weight),
            lambda: (stash_z, zeros_x),
        )
        if step_now > 0:
            stash_x = jnp.where(active, current, stash_x)
        if step_now + 1 < segments:
            current = hop(result, step_now, step_now + 1)
    stash_g = zeros_x
    upstream = cotangent
    for step_now in range(segments):
        owner = segments - 1 - step_now
        active = segment_index == owner
        held = upstream
        stash_g, passed = lax.cond(
            active,
            lambda: layer_backward(flat_cols, held, stash_z, weight),
            lambda: (stash_g, zeros_x),
        )
        if step_now + 1 < segments:
            upstream = hop(passed, owner, owner - 1)
    all_inputs = stash_x
    all_grads = stash_g
    ny, nx, nz = DP_SIZES
    members = ny
    group_pairs = num_blocks * per_block // members
    group_j = num_blocks // members
    member = lax.axis_index("y")
    grads_here = all_grads.reshape(all_rows, members, group_j * edge_size)
    pieces = [lax.dynamic_index_in_dim(grads_here, member, 1, False)]
    for offset in range(1, members):
        route = [(i, (i + offset) % members) for i in range(members)]
        outgoing = lax.dynamic_index_in_dim(grads_here, (member + offset) % members, 1, False)
        pieces.append(lax.ppermute(outgoing, "y", route))
    by_offset = jnp.stack(pieces)
    sender_offset = (member - jnp.arange(members, dtype=jnp.int32)) % members
    grads_group = jnp.take(by_offset, sender_offset, axis=0).reshape(
        members * all_rows, group_j * edge_size
    )
    inputs_group = lax.all_gather(all_inputs, "y", axis=0, tiled=True)
    cols_here = lax.dynamic_slice_in_dim(flat_cols, member * group_pairs, group_pairs)
    order = np.arange(group_pairs).reshape(nx, nz, -1).transpose(1, 0, 2).reshape(-1)
    j_index = jnp.asarray(order // per_block, jnp.int32)
    partial = group_grads(cols_here[order], j_index, inputs_group, grads_group, group_pairs, 64)
    reduced = ring_reduce_scatter(partial.reshape(nz, -1, edge_size), "z", nz)
    halves = reduced.reshape(nx, -1, edge_size)
    side = lax.axis_index("xlo")
    got = lax.ppermute(lax.dynamic_index_in_dim(halves, 1 - side, 0, False), "xlo", [(0, 1), (1, 0)])
    own_share = lax.dynamic_index_in_dim(halves, side, 0, False) + got
    summed = own_share.astype(jnp.bfloat16)
    return summed[None]


def solution(mesh):
    fine = Mesh(mesh.devices.reshape(mesh.shape["segment"], *DP_SIZES), ("segment",) + DP_AXES)
    return jax.shard_map(
        body,
        mesh=fine,
        in_specs=(
            P(DP_AXES, None),
            P(DP_AXES, None),
            P("segment", None, None, None, None),
            P("segment", None, None),
        ),
        out_specs=P("segment", DP_AXES, None),
        check_vma=False,
    )
```
